512 devices in a mesh: img: 128 (over y, z_lo, x), vol: 4 (over z_hi, core).
Axes of the slice: x: 4, y: 4, z: 16 (z_hi: 2, z_lo: 8; z = z_hi * 8 + z_lo), core: 2. Of those that a mesh axis runs over, the one named last changes fastest.
Arguments:
- images: bfloat16 [128, 400, 400], P('img'), may hold values from -6 to 6
- volume: bfloat16 [4, 32768, 400], P('vol', 'img'), may hold values from -6 to 6
- row_order: int32 [128, 8, 400], P('img'), may hold values from 0 to 399, each once within a row
- tap_owner: int32 [4, 128, 8, 200, 1], P('vol', 'img'), may hold values from 0 to 127; in each aligned block of 1600 rows (0 to 1599, 1600 to 3199, ..., all dimensions but the last counted through in order) at most 17 rows name the same one
- tap_local: int32 [4, 128, 8, 200], P('vol', 'img'), may hold values from 0 to 255
- interp_index: int32 [4, 128, 8, 100], P('vol', 'img'), may hold values from 0 to 63
- interp_table: float32 [64], replicated, may hold values from 0 to 1
- ctf_index: int32 [128], P('img'), may hold values from 0 to 15
- ctf_defocus: float32 [16], replicated, may hold values from 2.5e-05 to 0.00025
- ctf_phase: float32 [16], replicated, may hold values from 0 to 1.2
- noise_inv: float32 [128], P('img'), may hold values from 0.5 to 4
Outputs:
- data_sum: float32 [4, 32768, 400], P('vol', 'img')
- weight_sum: float32 [4, 32768, 200], P('vol', 'img')
- pose_weights: float32 [128, 8], P('img')
The draws below stay inside these ranges and needn't reach their ends.
Inputs may be any that keep to these rules, and one draw needn't show every extreme that they name: `tap_owner`: in each aligned block of 1600 tap rows (one block per slab and image shard), no owner is named more than 17 times.
All inputs are finite; a program needn't handle non-finite values.
Results may differ from the reference program's by a relative error of at most 0.007.
Values may be sent and summed in bfloat16 or wider, within the bound.
No kernel may reach another device: no remote copies, remote signals or barrier semaphores. Data moves between devices by JAX's collectives and lax.ppermute only.
A program may use at most 128 MiB of HBM per device.

```python
import math
import jax
import jax.numpy as jnp
import numpy as np
from jax import lax

K = 400
FREQ = 200
POSES = 8
IMG_DEV = 1
SR_DEV = 256
NCTF = 16
WTAB = 64
IMAGES = 128
SLABS = 4
SLAB_ROWS = 32768
QROWS = 100
CAP = 17
N_IMG = 128
N_VOL = 4


def set_ends(entries, stream_key, smallest, top_value):
    spot = [jax.random.randint(jax.random.fold_in(stream_key, axis), (), 0, length) for axis, length in enumerate(entries.shape)]
    main_axis = entries.shape.index(max(entries.shape))
    neighbour = spot[:main_axis] + [(spot[main_axis] + 1) % entries.shape[main_axis]] + spot[main_axis + 1:]
    return entries.at[tuple(spot)].set(smallest).at[tuple(neighbour)].set(top_value)


def level_of(stream_key, shape, pieces, smallest, largest):
    level, own = 1.0, jax.random.fold_in(stream_key, 6)
    for dim, parts in pieces:
        heights = jnp.exp(jax.random.uniform(jax.random.fold_in(own, dim), (parts,), jnp.float32, smallest / len(pieces), largest / len(pieces)))
        level = level * jnp.repeat(heights, shape[dim] // parts).reshape([-1 if axis == dim else 1 for axis in range(len(shape))])
    return level


def assign_block(key, own, number, rows, number_of, top, bound, skew):
    order = jax.random.permutation(key, number_of)
    crowded, ordinary = shares(number_of, rows * top, bound, skew, True), shares(number_of, rows * top, bound, skew, False)
    places = jnp.arange(number_of)

    def named(sizes, rotation):
        used = int((sizes > 0).sum())
        fixed = max(1, used // 4)
        moved = fixed + (places - fixed + rotation * (used - fixed)) % max(1, number_of - fixed)
        return jnp.zeros((number_of,), jnp.int32).at[order[jnp.where(places < fixed, places, moved)]].set(jnp.asarray(sizes, jnp.int32))

    sizes = jnp.where(number % 4 == 0, named(crowded, number // 4), named(ordinary, number - number // 4 - 1))
    mixed = jax.random.permutation(jax.random.fold_in(own, 3), number_of)
    giver, receiver = mixed[0:number_of // 2 * 2:2], mixed[1:number_of // 2 * 2:2]
    margin = jnp.minimum(sizes[giver] - 1, bound - sizes[receiver]) // 2
    margin = jnp.where((giver == order[0]) | (receiver == order[0]) | (sizes[receiver] == 0), 0, jnp.maximum(margin, 0))
    moved = jax.random.randint(jax.random.fold_in(own, 4), (number_of // 2,), 0, 1 << 20) % (margin + 1)
    sizes = sizes.at[giver].add(-moved).at[receiver].add(moved)
    labels = jnp.searchsorted(jnp.cumsum(sizes), jnp.arange(rows * top), side="right").astype(jnp.int32)
    listing = labels.reshape(top, rows).T
    listing = listing[jax.random.permutation(jax.random.fold_in(own, 1), rows)]
    rotation = jax.random.randint(jax.random.fold_in(own, 2), (rows, 1), 0, top)
    return jnp.take_along_axis(listing, (jnp.arange(top)[None, :] + rotation) % top, axis=1)


def shares(number_of, total, most, skew, full):
    weights = [(1 << 20) // math.isqrt(standing ** skew) + 1 for standing in range(1, number_of + 1)]
    largest = most if full else min(most, max(-(-total // number_of), total * weights[0] // sum(weights)))
    least = 1 if total - largest >= number_of - 1 else 0
    counts, rest = [largest] + [least] * (number_of - 1), total - largest - least * (number_of - 1)
    while rest > 0:
        free = [i for i in range(1, number_of) if counts[i] < largest] or [i for i in range(1, number_of) if counts[i] < most]
        pool, budget = sum([weights[i] for i in free]), rest
        for i in free:
            extra = min(most - counts[i], max(1, budget * weights[i] // pool), rest)
            counts[i] = counts[i] + extra
            rest = rest - extra
    return np.array(counts)


def noise(rng, extent, deviation, limit, pieces=(), held_as=jnp.bfloat16):
    array = jax.random.normal(rng, extent, jnp.float32) * deviation
    if len(pieces) > 0:
        array = level_of(rng, extent, pieces, -0.22, 0.18) * array
    return jnp.clip(array, min=-limit, max=limit).astype(held_as)


def setup_inputs(seed: int = 0) -> dict:
    streams_of = jax.random.split(jax.random.key(seed), 12)
    images = noise(streams_of[0], (IMAGES, K, K), 1.0, 6.0, ((0, 128),))
    volume = noise(streams_of[1], (SLABS, SLAB_ROWS, 2 * FREQ), 1.0, 6.0, ((0, 4), (1, 128)))
    row_order = jax.vmap(lambda own: jax.random.permutation(own, K))(jax.random.split(streams_of[2], IMAGES * POSES)).reshape((IMAGES, POSES, K)).astype(jnp.int32)
    tap_owner_keys = jax.random.split(jax.random.fold_in(streams_of[3], 1), SLABS * IMAGES * POSES * (2 * QROWS) // (IMG_DEV * POSES * 2 * QROWS))
    tap_owner_turns = jax.random.permutation(jax.random.fold_in(streams_of[3], 3), SLABS * IMAGES * POSES * (2 * QROWS) // (IMG_DEV * POSES * 2 * QROWS))
    tap_owner = jax.vmap(lambda own, number: assign_block(jax.random.fold_in(streams_of[3], 2), own, number, IMG_DEV * POSES * 2 * QROWS, N_IMG, 1, CAP, 0))(tap_owner_keys, tap_owner_turns).reshape((SLABS, IMAGES, POSES, 2 * QROWS, 1))
    tap_local = set_ends(jax.random.randint(streams_of[4], (SLABS, IMAGES, POSES, 2 * QROWS), 0, SR_DEV), jax.random.fold_in(streams_of[4], 1), 0, SR_DEV - 1).astype(jnp.int32)
    interp_index = set_ends(jax.random.randint(streams_of[5], (SLABS, IMAGES, POSES, QROWS), 0, WTAB), jax.random.fold_in(streams_of[5], 1), 0, WTAB - 1).astype(jnp.int32)
    interp_table = jnp.clip(jax.random.uniform(streams_of[6], (WTAB,), jnp.float32, 0.0, 1.0), 0.0, 1.0)
    ctf_index = set_ends(jax.random.randint(streams_of[7], (IMAGES,), 0, NCTF), jax.random.fold_in(streams_of[7], 1), 0, NCTF - 1).astype(jnp.int32)
    ctf_defocus = jnp.clip(jnp.exp(jax.random.uniform(streams_of[8], (NCTF,), jnp.float32, math.log(2.499999936844688e-05), math.log(0.00025))), 2.499999936844688e-05, 0.00025)
    ctf_phase = jnp.clip(jax.random.uniform(streams_of[9], (NCTF,), jnp.float32, 0.0, 1.2), 0.0, 1.2)
    noise_inv = jnp.clip(jnp.exp(math.log(4.0) - 2.0794415 * jax.random.uniform(streams_of[10], (IMAGES,), jnp.float32) ** level_of(streams_of[10], (IMAGES,), ((0, 128),), -0.2, 0.2)), 0.5, 4.0)
    return {"images": images, "volume": volume, "row_order": row_order, "tap_owner": tap_owner, "tap_local": tap_local, "interp_index": interp_index, "interp_table": interp_table, "ctf_index": ctf_index, "ctf_defocus": ctf_defocus, "ctf_phase": ctf_phase, "noise_inv": noise_inv}


def fourier_tables(size_k, size_f):
    positions = jnp.arange(size_k, dtype=jnp.int32)
    columns = jnp.arange(size_f, dtype=jnp.int32)
    scale_factor = 1.0 / math.sqrt(size_k)
    phase_x = (positions[:, None] * columns[None, :] % size_k).astype(jnp.float32) * (2.0 * math.pi / size_k)
    table_x = jnp.concatenate([jnp.cos(phase_x), -jnp.sin(phase_x)], axis=1) * scale_factor
    phase_y = (positions[:, None] * positions[None, :] % size_k).astype(jnp.float32) * (2.0 * math.pi / size_k)
    table_y = jnp.concatenate([jnp.cos(phase_y), jnp.sin(phase_y)], axis=1) * scale_factor
    return (table_x.astype(jnp.bfloat16), table_y.astype(jnp.bfloat16))

def contrast_rows(freq_rows, defocus, phase_shift, size_k, size_f):
    signed = jnp.where(freq_rows < size_k // 2, freq_rows, freq_rows - size_k)
    columns = jnp.arange(size_f, dtype=jnp.int32)
    radius = (signed * signed)[..., None] + columns * columns
    return -jnp.sin(defocus * radius.astype(jnp.float32) + phase_shift)

def slice_terms(tap_values, mixing, spec_rows, contrast):
    tap_float = tap_values.astype(jnp.float32)
    mix_weight = mixing[..., None]
    sliced = mix_weight * tap_float[..., 0, :] + (1.0 - mix_weight) * tap_float[..., 1, :]
    size_f = contrast.shape[-1]
    spec_float = spec_rows.astype(jnp.float32)
    cross_term = contrast * (spec_float[..., :size_f] * sliced[..., :size_f] + spec_float[..., size_f:] * sliced[..., size_f:])
    power_term = contrast * contrast * (sliced[..., :size_f] ** 2 + sliced[..., size_f:] ** 2)
    return lax.optimization_barrier(jnp.sum(cross_term - 0.5 * power_term, axis=(-2, -1)))

def coefficients(weight_col, mixing):
    return jnp.stack([mixing, 1.0 - mixing], axis=-1) * weight_col[..., None]

def deposits(tap_coef, contrast, spec_rows):
    scaled = tap_coef[..., None] * contrast[..., None, :]
    spec_float = spec_rows.astype(jnp.float32)[..., None, :]
    data_rows = (jnp.concatenate([scaled, scaled], axis=-1) * spec_float).astype(jnp.bfloat16)
    weight_rows = (scaled * contrast[..., None, :]).astype(jnp.bfloat16)
    return (data_rows, weight_rows)

def spectra_of(images):
    image_count, size_k, _ = images.shape
    size_f = size_k // 2
    table_x, table_y = fourier_tables(size_k, size_f)
    half_spec = jnp.dot(images.reshape(image_count * size_k, size_k), table_x, preferred_element_type=jnp.float32)
    half_spec = half_spec.astype(jnp.bfloat16).reshape(image_count, size_k, 2 * size_f)

    def one_image(image_item):
        other = jnp.concatenate([image_item[:, size_f:], -image_item[:, :size_f]], axis=1)
        stacked = jnp.concatenate([image_item, other], axis=0)
        return jnp.dot(table_y, stacked, preferred_element_type=jnp.float32).astype(jnp.bfloat16)
    return lax.map(one_image, half_spec)

def reference(images, volume, row_order, tap_owner, tap_local, interp_index, interp_table, ctf_index, ctf_defocus, ctf_phase, noise_inv):
    spectrum = spectra_of(images)
    defocus = ctf_defocus[ctf_index]
    phase_shift = ctf_phase[ctf_index]
    rows_all = jnp.swapaxes(tap_owner[..., 0] * SR_DEV + tap_local, 0, 1).astype(jnp.int32)
    mix_table = jnp.swapaxes(interp_table[interp_index], 0, 1)

    def score_one(image_item):
        spec_one, order_one, rows_one, mix_one, defo_one, shift_one = image_item
        score_sum = jnp.zeros((POSES,), jnp.float32)
        for slab in range(N_VOL):
            freq_rows = order_one[:, slab * QROWS:(slab + 1) * QROWS]
            spec_rows = spec_one[freq_rows]
            contrast = contrast_rows(freq_rows, defo_one, shift_one, K, FREQ)
            tap_values = volume[slab][rows_one[slab]].reshape(POSES, QROWS, 2, 2 * FREQ)
            score_sum = score_sum + slice_terms(tap_values, mix_one[slab], spec_rows, contrast)
        return score_sum
    totals = lax.map(score_one, (spectrum, row_order, rows_all, mix_table, defocus, phase_shift))
    scores = noise_inv[:, None] * totals * (1.0 / math.sqrt(K * FREQ))
    pose_weights = jax.nn.softmax(scores, axis=-1)

    def deposit_one(carry, image_item):
        data_acc, weight_acc = carry
        spec_one, order_one, rows_one, mix_one, defo_one, shift_one, weight_one = image_item
        for slab in range(N_VOL):
            freq_rows = order_one[:, slab * QROWS:(slab + 1) * QROWS]
            spec_rows = spec_one[freq_rows]
            contrast = contrast_rows(freq_rows, defo_one, shift_one, K, FREQ)
            tap_coef = coefficients(weight_one[:, None], mix_one[slab])
            data_rows, weight_rows = deposits(tap_coef, contrast, spec_rows)
            flat_rows = rows_one[slab].reshape(-1)
            data_acc = data_acc.at[slab, flat_rows].add(data_rows.reshape(-1, 2 * FREQ).astype(jnp.float32))
            weight_acc = weight_acc.at[slab, flat_rows].add(weight_rows.reshape(-1, FREQ).astype(jnp.float32))
        return ((data_acc, weight_acc), None)
    start_acc = (jnp.zeros((SLABS, SLAB_ROWS, 2 * FREQ), jnp.float32), jnp.zeros((SLABS, SLAB_ROWS, FREQ), jnp.float32))
    (data_sum, weight_sum), _ = lax.scan(deposit_one, start_acc, (spectrum, row_order, rows_all, mix_table, defocus, phase_shift, pose_weights))
    return (data_sum, weight_sum, pose_weights)
```

```python
import math

import jax
import jax.numpy as jnp
from jax import lax
from jax.sharding import PartitionSpec as P


def fourier_tables(size_k, size_f):
    positions = jnp.arange(size_k, dtype=jnp.int32)
    columns = jnp.arange(size_f, dtype=jnp.int32)
    scale_factor = 1.0 / math.sqrt(size_k)
    phase_x = (positions[:, None] * columns[None, :] % size_k).astype(jnp.float32) * (
        2.0 * math.pi / size_k
    )
    table_x = jnp.concatenate([jnp.cos(phase_x), -jnp.sin(phase_x)], axis=1) * scale_factor
    phase_y = (positions[:, None] * positions[None, :] % size_k).astype(jnp.float32) * (
        2.0 * math.pi / size_k
    )
    table_y = jnp.concatenate([jnp.cos(phase_y), jnp.sin(phase_y)], axis=1) * scale_factor
    return (table_x.astype(jnp.bfloat16), table_y.astype(jnp.bfloat16))


def contrast_of(radius_sq, defocus, phase_shift, size_f):
    columns = jnp.arange(size_f, dtype=jnp.int32)
    radius = radius_sq[..., None] + columns * columns
    return -jnp.sin(defocus * radius.astype(jnp.float32) + phase_shift)


def slice_terms(tap_values, mixing, spec_rows, contrast):
    tap_float = tap_values.astype(jnp.float32)
    mix_weight = mixing[..., None]
    sliced = mix_weight * tap_float[..., 0, :] + (1.0 - mix_weight) * tap_float[..., 1, :]
    size_f = contrast.shape[-1]
    spec_float = spec_rows.astype(jnp.float32)
    cross_term = contrast * (
        spec_float[..., :size_f] * sliced[..., :size_f]
        + spec_float[..., size_f:] * sliced[..., size_f:]
    )
    power_term = contrast * contrast * (sliced[..., :size_f] ** 2 + sliced[..., size_f:] ** 2)
    return jnp.sum(cross_term - 0.5 * power_term, axis=(-2, -1))


def half_transform(images, table_x):
    return jnp.einsum("iyx,xc->iyc", images, table_x, preferred_element_type=jnp.float32).astype(
        jnp.bfloat16
    )


def full_transform(half_spec, table_y, width):
    other = jnp.concatenate([half_spec[..., width:], -half_spec[..., :width]], axis=-1)
    stacked = jnp.concatenate([half_spec, other], axis=1)
    return jnp.einsum("uy,iyc->iuc", table_y, stacked, preferred_element_type=jnp.float32).astype(
        jnp.bfloat16
    )


def small_lookup(index_rows, table):
    entries = jnp.arange(table.shape[0], dtype=jnp.int32)
    return jnp.sum(
        jnp.where(index_rows[..., None] == entries, table, jnp.zeros_like(table)), axis=-1
    )


def one_hot(index, count):
    return (index[..., None] == jnp.arange(count, dtype=jnp.int32)).astype(jnp.bfloat16)


def exchange(blocks):
    peers, cap, width = blocks.shape
    per_peer = cap * width
    tile = 16 * 128
    padded = -(-per_peer // tile) * tile
    flat = jnp.pad(blocks.reshape(peers, per_peer), ((0, 0), (0, padded - per_peer)))
    moved = lax.all_to_all(
        flat.reshape(peers, padded // 128, 128), "img", split_axis=0, concat_axis=0, tiled=True
    )
    return moved.reshape(peers, padded)[:, :per_peer].reshape(peers, cap, width)


def body(
    images,
    volume,
    row_order,
    tap_owner,
    tap_local,
    interp_index,
    interp_table,
    ctf_index,
    ctf_defocus,
    ctf_phase,
    noise_inv,
):
    f32, bf16, i32 = jnp.float32, jnp.bfloat16, jnp.int32
    image_count, size_k, _ = images.shape
    size_f = size_k // 2
    width = 2 * size_f
    pose_count = row_order.shape[1]
    vol_count = lax.axis_size("vol")
    img_count = lax.axis_size("img")
    quarter = size_k // vol_count
    slab_rows = volume.shape[1]
    slab_index = lax.axis_index("vol")
    img_index = lax.axis_index("img")

    table_x, table_y = fourier_tables(size_k, size_f)
    half_spec = half_transform(images, table_x)
    spectrum = full_transform(half_spec, table_y, size_f)
    freq_rows = lax.dynamic_slice_in_dim(row_order, slab_index * quarter, quarter, 2)
    spec_rows = jnp.einsum(
        "ipqu,iuc->ipqc", one_hot(freq_rows, size_k), spectrum, preferred_element_type=f32
    ).astype(bf16)

    owners = tap_owner[0, ..., 0].reshape(-1)
    local_rows = tap_local[0].reshape(-1)
    request_count = owners.shape[0]
    capacity = request_count * 6 // (5 * img_count) + 2
    slot_count = img_count * capacity
    owner_hot = one_hot(owners, img_count)
    order = jnp.arange(request_count, dtype=i32)
    before = (order[None, :] < order[:, None]).astype(bf16)
    earlier = jnp.dot(before, owner_hot, preferred_element_type=f32)
    rank = jnp.sum(earlier * owner_hot.astype(f32), axis=1).astype(i32)
    slot_hot = one_hot(owners * capacity + rank, slot_count)

    signed_abs = jnp.where(freq_rows < size_f, freq_rows, size_k - freq_rows)
    per_row = lambda a: jnp.repeat(a.reshape(image_count, pose_count, quarter, 1), 2, axis=3)
    pose_ids = jnp.broadcast_to(
        jnp.arange(pose_count, dtype=i32)[None, :, None, None], (image_count, pose_count, quarter, 2)
    )
    tap_ids = jnp.broadcast_to(
        jnp.arange(2, dtype=i32)[None, None, None, :], (image_count, pose_count, quarter, 2)
    )
    image_ids = jnp.broadcast_to(
        jnp.arange(image_count, dtype=i32)[:, None, None, None], (image_count, pose_count, quarter, 2)
    )
    ctf_ids = jnp.broadcast_to(ctf_index[:, None, None, None], (image_count, pose_count, quarter, 2))
    meta = jnp.stack(
        [
            local_rows.reshape(image_count, pose_count, quarter, 2),
            per_row(signed_abs),
            pose_ids,
            per_row(interp_index[0]),
            tap_ids,
            jnp.ones_like(tap_ids),
            ctf_ids,
            image_ids,
        ],
        axis=-1,
    ).reshape(request_count, -1)
    meta_count = meta.shape[1]
    tap_spec = jnp.broadcast_to(
        spec_rows[:, :, :, None, :], (image_count, pose_count, quarter, 2, width)
    ).reshape(request_count, width)
    payload = jnp.concatenate([tap_spec, meta.astype(bf16)], axis=1)
    outgoing = jnp.einsum("js,jw->sw", slot_hot, payload, preferred_element_type=f32).astype(bf16)
    incoming = exchange(outgoing.reshape(img_count, capacity, width + meta_count)).reshape(
        slot_count, width + meta_count
    )

    got = incoming[:, width:].astype(f32).astype(i32)
    got_local, got_abs, got_pose, got_interp = got[:, 0], got[:, 1], got[:, 2], got[:, 3]
    got_tap, got_valid, got_ctf, got_image = got[:, 4], got[:, 5], got[:, 6], got[:, 7]
    row_hot = one_hot(jnp.where(got_valid > 0, got_local, slab_rows), slab_rows)
    found = jnp.dot(row_hot, volume[0], preferred_element_type=f32).astype(bf16)
    returned = exchange(found.reshape(img_count, capacity, width)).reshape(slot_count, width)

    tap_values = jnp.einsum("js,sw->jw", slot_hot, returned, preferred_element_type=f32).astype(bf16)
    tap_values = tap_values.reshape(image_count, pose_count, quarter, 2, width)
    defocus = small_lookup(ctf_index, ctf_defocus)[:, None, None, None]
    phase_shift = small_lookup(ctf_index, ctf_phase)[:, None, None, None]
    contrast = contrast_of(signed_abs * signed_abs, defocus, phase_shift, size_f)
    mixing = small_lookup(interp_index[0], interp_table)
    partial_value = slice_terms(tap_values, mixing, spec_rows, contrast)

    total_images = img_count * image_count
    noise_col = jnp.where(slab_index == 0, noise_inv, jnp.zeros_like(noise_inv))
    block = jnp.concatenate([partial_value, noise_col[:, None]], axis=1)
    placed = lax.dynamic_update_slice(
        jnp.zeros((total_images, pose_count + 1), f32), block, (img_index * image_count, 0)
    )
    summed = lax.psum(placed, ("img", "vol"))
    scores_all = (
        summed[:, pose_count][:, None]
        * summed[:, :pose_count]
        * (1.0 / math.sqrt(size_k * size_f))
    )
    weights_all = jax.nn.softmax(scores_all, axis=-1)
    pose_weights = lax.dynamic_slice_in_dim(weights_all, img_index * image_count, image_count, 0)

    by_peer = weights_all.reshape(img_count, 1, image_count * pose_count)
    combo = (got_image * pose_count + got_pose).reshape(img_count, capacity)
    weight_of = jnp.sum(
        jnp.where(
            combo[..., None] == jnp.arange(image_count * pose_count, dtype=i32), by_peer, 0.0
        ),
        axis=-1,
    ).reshape(slot_count)
    mix_of = small_lookup(got_interp, interp_table)
    mix_k = jnp.where(got_tap == 0, mix_of, 1.0 - mix_of)
    coef = mix_k * weight_of
    got_contrast = contrast_of(
        got_abs * got_abs,
        small_lookup(got_ctf, ctf_defocus)[:, None],
        small_lookup(got_ctf, ctf_phase)[:, None],
        size_f,
    )
    scaled = coef[:, None] * got_contrast
    spec_float = incoming[:, :width].astype(f32)
    data_rows = (jnp.concatenate([scaled, scaled], axis=-1) * spec_float).astype(bf16)
    weight_rows = (scaled * got_contrast).astype(bf16)
    data_acc = jnp.einsum("sr,sw->rw", row_hot, data_rows, preferred_element_type=f32)
    weight_acc = jnp.einsum("sr,sw->rw", row_hot, weight_rows, preferred_element_type=f32)
    return (data_acc[None], weight_acc[None], pose_weights)


def solution(mesh):
    placed = (
        P("img", None, None),
        P("vol", "img", None),
        P("img", None, None),
        P("vol", "img", None, None, None),
        P("vol", "img", None, None),
        P("vol", "img", None, None),
        P(),
        P("img"),
        P(),
        P(),
        P("img"),
    )
    return jax.shard_map(
        body,
        mesh=mesh,
        in_specs=placed,
        out_specs=(P("vol", "img", None), P("vol", "img", None), P("img", None)),
        check_vma=False,
    )
```

```python
import math

import jax
import jax.numpy as jnp
from jax import lax
from jax.sharding import PartitionSpec as P


def fourier_tables(size_k, size_f):
    positions = jnp.arange(size_k, dtype=jnp.int32)
    columns = jnp.arange(size_f, dtype=jnp.int32)
    scale_factor = 1.0 / math.sqrt(size_k)
    phase_x = (positions[:, None] * columns[None, :] % size_k).astype(jnp.float32) * (
        2.0 * math.pi / size_k
    )
    table_x = jnp.concatenate([jnp.cos(phase_x), -jnp.sin(phase_x)], axis=1) * scale_factor
    phase_y = (positions[:, None] * positions[None, :] % size_k).astype(jnp.float32) * (
        2.0 * math.pi / size_k
    )
    table_y = jnp.concatenate([jnp.cos(phase_y), jnp.sin(phase_y)], axis=1) * scale_factor
    return (table_x.astype(jnp.bfloat16), table_y.astype(jnp.bfloat16))


def contrast_of(radius_sq, defocus, phase_shift, size_f):
    columns = jnp.arange(size_f, dtype=jnp.int32)
    radius = radius_sq[..., None] + columns * columns
    return -jnp.sin(defocus * radius.astype(jnp.float32) + phase_shift)


def half_transform(images, table_x):
    return jnp.einsum("iyx,xc->iyc", images, table_x, preferred_element_type=jnp.float32).astype(
        jnp.bfloat16
    )


def full_transform(half_spec, table_y, width):
    other = jnp.concatenate([half_spec[..., width:], -half_spec[..., :width]], axis=-1)
    stacked = jnp.concatenate([half_spec, other], axis=1)
    return jnp.einsum("uy,iyc->iuc", table_y, stacked, preferred_element_type=jnp.float32).astype(
        jnp.bfloat16
    )


def small_lookup(index_rows, table):
    entries = jnp.arange(table.shape[0], dtype=jnp.int32)
    return jnp.sum(
        jnp.where(index_rows[..., None] == entries, table, jnp.zeros_like(table)), axis=-1
    )


def one_hot(index, count):
    return (index[..., None] == jnp.arange(count, dtype=jnp.int32)).astype(jnp.bfloat16)


def exchange(parts):
    peers = parts[0].shape[0]
    flats = [part.reshape(peers, -1) for part in parts]
    sizes = [flat.shape[1] for flat in flats]
    used = sum(sizes)
    tile = 16 * 128
    padded = -(-used // tile) * tile
    flats.append(jnp.zeros((peers, padded - used), parts[0].dtype))
    packed = jnp.concatenate(flats, axis=1).reshape(peers, padded // 128, 128)
    moved = lax.all_to_all(packed, "img", split_axis=0, concat_axis=0, tiled=True)
    moved = moved.reshape(peers, padded)
    outs, offset = [], 0
    for part, size in zip(parts, sizes):
        outs.append(moved[:, offset : offset + size].reshape(part.shape))
        offset += size
    return outs


def body(
    images,
    volume,
    row_order,
    tap_owner,
    tap_local,
    interp_index,
    interp_table,
    ctf_index,
    ctf_defocus,
    ctf_phase,
    noise_inv,
):
    f32, bf16, i32 = jnp.float32, jnp.bfloat16, jnp.int32
    image_count, size_k, _ = images.shape
    size_f = size_k // 2
    width = 2 * size_f
    pose_count = row_order.shape[1]
    vol_count = lax.axis_size("vol")
    img_count = lax.axis_size("img")
    quarter = size_k // vol_count
    slab_rows = volume.shape[1]
    slab_index = lax.axis_index("vol")
    row_count = image_count * pose_count * quarter

    table_x, table_y = fourier_tables(size_k, size_f)
    half_spec = half_transform(images, table_x)
    spectrum = full_transform(half_spec, table_y, size_f)
    freq_rows = lax.dynamic_slice_in_dim(row_order, slab_index * quarter, quarter, 2)
    spec_rows = jnp.einsum(
        "ipqu,iuc->ipqc", one_hot(freq_rows, size_k), spectrum, preferred_element_type=f32
    ).astype(bf16).reshape(row_count, width)

    owners = tap_owner[0, ..., 0].reshape(-1)
    local_rows = tap_local[0].reshape(-1)
    request_count = owners.shape[0]
    capacity = request_count * 6 // (5 * img_count) + 2
    slot_count = img_count * capacity
    owner_hot = one_hot(owners, img_count)
    order = jnp.arange(request_count, dtype=i32)
    before = (order[None, :] < order[:, None]).astype(bf16)
    earlier = jnp.dot(before, owner_hot, preferred_element_type=f32)
    rank = jnp.sum(earlier * owner_hot.astype(f32), axis=1).astype(i32)
    slot_of = owners * capacity + rank
    slot_pair = slot_of.reshape(row_count, 2)
    slots = jnp.arange(slot_count, dtype=i32)
    pick_even = (slot_pair[:, 0:1] == slots[None, :]).astype(bf16)
    pick_odd = (slot_pair[:, 1:2] == slots[None, :]).astype(bf16)
    slot_hot_t = (slots[:, None] == slot_of[None, :]).astype(bf16)
    row_of_slot = (
        (slots[:, None] == slot_pair[None, :, 0]) | (slots[:, None] == slot_pair[None, :, 1])
    ).astype(bf16)

    signed_abs = jnp.where(freq_rows < size_f, freq_rows, size_k - freq_rows)
    shape4 = (image_count, pose_count, quarter, 2)
    per_row = lambda a: jnp.broadcast_to(a.reshape(image_count, pose_count, quarter, 1), shape4)
    pose_ids = jnp.broadcast_to(jnp.arange(pose_count, dtype=i32)[None, :, None, None], shape4)
    tap_ids = jnp.broadcast_to(jnp.arange(2, dtype=i32)[None, None, None, :], shape4)
    image_ids = jnp.broadcast_to(jnp.arange(image_count, dtype=i32)[:, None, None, None], shape4)
    ctf_ids = jnp.broadcast_to(ctf_index[:, None, None, None], shape4)
    meta = jnp.stack(
        [
            local_rows.reshape(shape4),
            per_row(signed_abs),
            pose_ids,
            per_row(interp_index[0]),
            tap_ids,
            jnp.ones_like(tap_ids),
            ctf_ids,
            image_ids,
        ],
        axis=-1,
    ).reshape(request_count, -1).astype(bf16)
    meta_count = meta.shape[1]
    send_spec = jnp.dot(row_of_slot, spec_rows, preferred_element_type=f32).astype(bf16)
    send_meta = jnp.dot(slot_hot_t, meta, preferred_element_type=f32).astype(bf16)
    got_spec, got_meta = exchange(
        [send_spec.reshape(img_count, capacity, width), send_meta.reshape(img_count, capacity, meta_count)]
    )
    got_spec = got_spec.reshape(slot_count, width)
    got = got_meta.reshape(slot_count, meta_count).astype(f32).astype(i32)

    got_local, got_abs, got_pose, got_interp = got[:, 0], got[:, 1], got[:, 2], got[:, 3]
    got_tap, got_valid, got_ctf, got_image = got[:, 4], got[:, 5], got[:, 6], got[:, 7]
    row_hot = one_hot(jnp.where(got_valid > 0, got_local, slab_rows), slab_rows)
    found = jnp.dot(row_hot, volume[0], preferred_element_type=f32).astype(bf16)
    (returned,) = exchange([found.reshape(img_count, capacity, width)])
    returned = returned.reshape(slot_count, width)

    defocus = small_lookup(ctf_index, ctf_defocus)[:, None, None, None]
    phase_shift = small_lookup(ctf_index, ctf_phase)[:, None, None, None]
    contrast = contrast_of(signed_abs * signed_abs, defocus, phase_shift, size_f).reshape(
        row_count, size_f
    )
    got_contrast = contrast_of(
        got_abs * got_abs,
        small_lookup(got_ctf, ctf_defocus)[:, None],
        small_lookup(got_ctf, ctf_phase)[:, None],
        size_f,
    )
    returned, contrast, got_contrast = lax.optimization_barrier((returned, contrast, got_contrast))

    tap_even = jnp.dot(pick_even, returned, preferred_element_type=f32).astype(bf16).astype(f32)
    tap_odd = jnp.dot(pick_odd, returned, preferred_element_type=f32).astype(bf16).astype(f32)
    mixing = small_lookup(interp_index[0], interp_table).reshape(row_count, 1)
    sliced = mixing * tap_even + (1.0 - mixing) * tap_odd
    spec_float = spec_rows.astype(f32)
    cross_term = contrast * (
        spec_float[:, :size_f] * sliced[:, :size_f] + spec_float[:, size_f:] * sliced[:, size_f:]
    )
    power_term = contrast * contrast * (sliced[:, :size_f] ** 2 + sliced[:, size_f:] ** 2)
    partial_value = jnp.sum(
        (cross_term - 0.5 * power_term).reshape(image_count, pose_count, quarter * size_f), axis=-1
    )
    score_sum = lax.psum(partial_value, "vol")
    scores = noise_inv[:, None] * score_sum * (1.0 / math.sqrt(size_k * size_f))
    pose_weights = jax.nn.softmax(scores, axis=-1)

    by_peer = lax.all_to_all(
        jnp.broadcast_to(pose_weights.reshape(1, 1, -1), (img_count, 1, image_count * pose_count)),
        "img",
        split_axis=0,
        concat_axis=0,
        tiled=True,
    )
    combo = (got_image * pose_count + got_pose).reshape(img_count, capacity)
    weight_of = jnp.sum(
        jnp.where(
            combo[..., None] == jnp.arange(image_count * pose_count, dtype=i32), by_peer, 0.0
        ),
        axis=-1,
    ).reshape(slot_count)
    mix_of = small_lookup(got_interp, interp_table)
    mix_k = jnp.where(got_tap == 0, mix_of, 1.0 - mix_of)
    coef = mix_k * weight_of
    scaled = coef[:, None] * got_contrast
    got_float = got_spec.astype(f32)
    data_rows = (jnp.concatenate([scaled, scaled], axis=-1) * got_float).astype(bf16)
    weight_rows = (scaled * got_contrast).astype(bf16)
    data_acc = jnp.einsum("sr,sw->rw", row_hot, data_rows, preferred_element_type=f32)
    weight_acc = jnp.einsum("sr,sw->rw", row_hot, weight_rows, preferred_element_type=f32)
    return (data_acc[None], weight_acc[None], pose_weights)


def solution(mesh):
    placed = (
        P("img", None, None),
        P("vol", "img", None),
        P("img", None, None),
        P("vol", "img", None, None, None),
        P("vol", "img", None, None),
        P("vol", "img", None, None),
        P(),
        P("img"),
        P(),
        P(),
        P("img"),
    )
    return jax.shard_map(
        body,
        mesh=mesh,
        in_specs=placed,
        out_specs=(P("vol", "img", None), P("vol", "img", None), P("img", None)),
        check_vma=False,
    )
```

```python
import math

import jax
import jax.numpy as jnp
from jax import lax
from jax.sharding import PartitionSpec as P


def fourier_tables(size_k, size_f):
    positions = jnp.arange(size_k, dtype=jnp.int32)
    columns = jnp.arange(size_f, dtype=jnp.int32)
    scale_factor = 1.0 / math.sqrt(size_k)
    phase_x = (positions[:, None] * columns[None, :] % size_k).astype(jnp.float32) * (
        2.0 * math.pi / size_k
    )
    table_x = jnp.concatenate([jnp.cos(phase_x), -jnp.sin(phase_x)], axis=1) * scale_factor
    phase_y = (positions[:, None] * positions[None, :] % size_k).astype(jnp.float32) * (
        2.0 * math.pi / size_k
    )
    table_y = jnp.concatenate([jnp.cos(phase_y), jnp.sin(phase_y)], axis=1) * scale_factor
    return (table_x.astype(jnp.bfloat16), table_y.astype(jnp.bfloat16))


def contrast_of(radius_sq, defocus, phase_shift, size_f):
    columns = jnp.arange(size_f, dtype=jnp.int32)
    radius = radius_sq[..., None] + columns * columns
    return -jnp.sin(defocus * radius.astype(jnp.float32) + phase_shift)


def half_transform(images, table_x):
    return jnp.einsum("iyx,xc->iyc", images, table_x, preferred_element_type=jnp.float32).astype(
        jnp.bfloat16
    )


def full_transform(half_spec, table_y, width):
    other = jnp.concatenate([half_spec[..., width:], -half_spec[..., :width]], axis=-1)
    stacked = jnp.concatenate([half_spec, other], axis=1)
    return jnp.einsum("uy,iyc->iuc", table_y, stacked, preferred_element_type=jnp.float32).astype(
        jnp.bfloat16
    )


def small_lookup(index_rows, table):
    entries = jnp.arange(table.shape[0], dtype=jnp.int32)
    return jnp.sum(
        jnp.where(index_rows[..., None] == entries, table, jnp.zeros_like(table)), axis=-1
    )


def one_hot(index, count):
    return (index[..., None] == jnp.arange(count, dtype=jnp.int32)).astype(jnp.bfloat16)


def exchange(parts, after=None):
    peers = parts[0].shape[0]
    flats = [part.reshape(peers, -1) for part in parts]
    sizes = [flat.shape[1] for flat in flats]
    used = sum(sizes)
    tile = 16 * 128
    padded = -(-used // tile) * tile
    flats.append(jnp.zeros((peers, padded - used), parts[0].dtype))
    packed = jnp.concatenate(flats, axis=1).reshape(peers, padded // 128, 128)
    if after is not None:
        packed, _ = lax.optimization_barrier((packed, after))
    moved = lax.all_to_all(packed, "img", split_axis=0, concat_axis=0, tiled=True)
    moved = moved.reshape(peers, padded)
    outs, offset = [], 0
    for part, size in zip(parts, sizes):
        outs.append(moved[:, offset : offset + size].reshape(part.shape))
        offset += size
    return outs


def body(
    images,
    volume,
    row_order,
    tap_owner,
    tap_local,
    interp_index,
    interp_table,
    ctf_index,
    ctf_defocus,
    ctf_phase,
    noise_inv,
):
    f32, bf16, i32 = jnp.float32, jnp.bfloat16, jnp.int32
    image_count, size_k, _ = images.shape
    size_f = size_k // 2
    width = 2 * size_f
    pose_count = row_order.shape[1]
    vol_count = lax.axis_size("vol")
    img_count = lax.axis_size("img")
    quarter = size_k // vol_count
    slab_rows = volume.shape[1]
    slab_index = lax.axis_index("vol")
    row_count = image_count * pose_count * quarter

    table_x, table_y = fourier_tables(size_k, size_f)
    half_spec = half_transform(images, table_x)
    spectrum = full_transform(half_spec, table_y, size_f)
    freq_rows = lax.dynamic_slice_in_dim(row_order, slab_index * quarter, quarter, 2)
    spec_rows = jnp.einsum(
        "ipqu,iuc->ipqc", one_hot(freq_rows, size_k), spectrum, preferred_element_type=f32
    ).astype(bf16).reshape(row_count, width)

    owners = tap_owner[0, ..., 0].reshape(-1)
    local_rows = tap_local[0].reshape(-1)
    request_count = owners.shape[0]
    capacity = request_count * 6 // (5 * img_count) + 2
    slot_count = img_count * capacity
    owner_hot = one_hot(owners, img_count)
    order = jnp.arange(request_count, dtype=i32)
    before = (order[None, :] < order[:, None]).astype(bf16)
    earlier = jnp.dot(before, owner_hot, preferred_element_type=f32)
    rank = jnp.sum(earlier * owner_hot.astype(f32), axis=1).astype(i32)
    slot_of = owners * capacity + rank
    slot_pair = slot_of.reshape(row_count, 2)
    slots = jnp.arange(slot_count, dtype=i32)
    pick_even = (slot_pair[:, 0:1] == slots[None, :]).astype(bf16)
    pick_odd = (slot_pair[:, 1:2] == slots[None, :]).astype(bf16)
    slot_hot_t = (slots[:, None] == slot_of[None, :]).astype(bf16)
    row_of_slot = (
        (slots[:, None] == slot_pair[None, :, 0]) | (slots[:, None] == slot_pair[None, :, 1])
    ).astype(bf16)

    signed_abs = jnp.where(freq_rows < size_f, freq_rows, size_k - freq_rows)
    shape4 = (image_count, pose_count, quarter, 2)
    per_row = lambda a: jnp.broadcast_to(a.reshape(image_count, pose_count, quarter, 1), shape4)
    pose_ids = jnp.broadcast_to(jnp.arange(pose_count, dtype=i32)[None, :, None, None], shape4)
    tap_ids = jnp.broadcast_to(jnp.arange(2, dtype=i32)[None, None, None, :], shape4)
    image_ids = jnp.broadcast_to(jnp.arange(image_count, dtype=i32)[:, None, None, None], shape4)
    ctf_ids = jnp.broadcast_to(ctf_index[:, None, None, None], shape4)
    meta = jnp.stack(
        [
            local_rows.reshape(shape4),
            per_row(signed_abs),
            pose_ids,
            per_row(interp_index[0]),
            tap_ids,
            jnp.ones_like(tap_ids),
            ctf_ids,
            image_ids,
        ],
        axis=-1,
    ).reshape(request_count, -1).astype(bf16)
    meta_count = meta.shape[1]
    send_spec = jnp.dot(row_of_slot, spec_rows, preferred_element_type=f32).astype(bf16)
    fields = jnp.dot(slot_hot_t, meta, preferred_element_type=f32).astype(i32)
    word_a = (fields[:, 0] + 1) * fields[:, 5] + (slab_rows + 1) * (
        fields[:, 1] + (size_f + 1) * fields[:, 6]
    )
    word_b = fields[:, 2] + pose_count * (
        fields[:, 3] + interp_table.shape[0] * (fields[:, 4] + 2 * fields[:, 7])
    )
    words = jnp.stack(
        [word_a.reshape(img_count, capacity), word_b.reshape(img_count, capacity)], axis=1
    ).reshape(img_count, 1, 2 * capacity)
    got_words = lax.all_to_all(words, "img", split_axis=0, concat_axis=0, tiled=True).reshape(
        img_count, 2, capacity
    )
    word_a = got_words[:, 0, :].reshape(-1)
    word_b = got_words[:, 1, :].reshape(-1)
    got_local = word_a % (slab_rows + 1) - 1
    rest = word_a // (slab_rows + 1)
    got_abs = rest % (size_f + 1)
    got_ctf = rest // (size_f + 1)
    got_pose = word_b % pose_count
    rest = word_b // pose_count
    got_interp = rest % interp_table.shape[0]
    rest = rest // interp_table.shape[0]
    got_tap = rest % 2
    got_image = rest // 2

    row_hot = one_hot(jnp.where(got_local >= 0, got_local, slab_rows), slab_rows)
    found = jnp.dot(row_hot, volume[0], preferred_element_type=f32).astype(bf16)
    (returned,) = exchange([found.reshape(img_count, capacity, width)])
    returned = returned.reshape(slot_count, width)

    (got_spec,) = exchange([send_spec.reshape(img_count, capacity, width)], after=returned)
    got_spec = got_spec.reshape(slot_count, width)

    defocus = small_lookup(ctf_index, ctf_defocus)[:, None, None, None]
    phase_shift = small_lookup(ctf_index, ctf_phase)[:, None, None, None]
    contrast = contrast_of(signed_abs * signed_abs, defocus, phase_shift, size_f).reshape(
        row_count, size_f
    )
    got_contrast = contrast_of(
        got_abs * got_abs,
        small_lookup(got_ctf, ctf_defocus)[:, None],
        small_lookup(got_ctf, ctf_phase)[:, None],
        size_f,
    )
    returned, contrast, got_contrast = lax.optimization_barrier((returned, contrast, got_contrast))

    tap_even = jnp.dot(pick_even, returned, preferred_element_type=f32).astype(bf16).astype(f32)
    tap_odd = jnp.dot(pick_odd, returned, preferred_element_type=f32).astype(bf16).astype(f32)
    mixing = small_lookup(interp_index[0], interp_table).reshape(row_count, 1)
    sliced = mixing * tap_even + (1.0 - mixing) * tap_odd
    spec_float = spec_rows.astype(f32)
    cross_term = contrast * (
        spec_float[:, :size_f] * sliced[:, :size_f] + spec_float[:, size_f:] * sliced[:, size_f:]
    )
    power_term = contrast * contrast * (sliced[:, :size_f] ** 2 + sliced[:, size_f:] ** 2)
    partial_value = jnp.sum(
        (cross_term - 0.5 * power_term).reshape(image_count, pose_count, quarter * size_f), axis=-1
    )
    score_sum = lax.psum(partial_value, "vol")
    scores = noise_inv[:, None] * score_sum * (1.0 / math.sqrt(size_k * size_f))
    pose_weights = jax.nn.softmax(scores, axis=-1)

    by_peer = lax.all_gather(pose_weights.reshape(1, -1), "img", axis=0, tiled=True).reshape(
        img_count, 1, image_count * pose_count
    )
    combo = (got_image * pose_count + got_pose).reshape(img_count, capacity)
    weight_of = jnp.sum(
        jnp.where(
            combo[..., None] == jnp.arange(image_count * pose_count, dtype=i32), by_peer, 0.0
        ),
        axis=-1,
    ).reshape(slot_count)
    mix_of = small_lookup(got_interp, interp_table)
    mix_k = jnp.where(got_tap == 0, mix_of, 1.0 - mix_of)
    coef = mix_k * weight_of
    scaled = coef[:, None] * got_contrast
    got_float = got_spec.astype(f32)
    data_rows = (jnp.concatenate([scaled, scaled], axis=-1) * got_float).astype(bf16)
    weight_rows = (scaled * got_contrast).astype(bf16)
    data_acc = jnp.einsum("sr,sw->rw", row_hot, data_rows, preferred_element_type=f32)
    weight_acc = jnp.einsum("sr,sw->rw", row_hot, weight_rows, preferred_element_type=f32)
    return (data_acc[None], weight_acc[None], pose_weights)


def solution(mesh):
    placed = (
        P("img", None, None),
        P("vol", "img", None),
        P("img", None, None),
        P("vol", "img", None, None, None),
        P("vol", "img", None, None),
        P("vol", "img", None, None),
        P(),
        P("img"),
        P(),
        P(),
        P("img"),
    )
    return jax.shard_map(
        body,
        mesh=mesh,
        in_specs=placed,
        out_specs=(P("vol", "img", None), P("vol", "img", None), P("img", None)),
        check_vma=False,
    )
```

```python
import math

import jax
import jax.numpy as jnp
from jax import lax
from jax.sharding import PartitionSpec as P


def fourier_tables(size_k, size_f):
    positions = jnp.arange(size_k, dtype=jnp.int32)
    columns = jnp.arange(size_f, dtype=jnp.int32)
    scale_factor = 1.0 / math.sqrt(size_k)
    phase_x = (positions[:, None] * columns[None, :] % size_k).astype(jnp.float32) * (
        2.0 * math.pi / size_k
    )
    table_x = jnp.concatenate([jnp.cos(phase_x), -jnp.sin(phase_x)], axis=1) * scale_factor
    phase_y = (positions[:, None] * positions[None, :] % size_k).astype(jnp.float32) * (
        2.0 * math.pi / size_k
    )
    table_y = jnp.concatenate([jnp.cos(phase_y), jnp.sin(phase_y)], axis=1) * scale_factor
    return (table_x.astype(jnp.bfloat16), table_y.astype(jnp.bfloat16))


def contrast_of(radius_sq, defocus, phase_shift, size_f):
    columns = jnp.arange(size_f, dtype=jnp.int32)
    radius = radius_sq[..., None] + columns * columns
    return -jnp.sin(defocus * radius.astype(jnp.float32) + phase_shift)


def half_transform(images, table_x):
    return jnp.einsum("iyx,xc->iyc", images, table_x, preferred_element_type=jnp.float32).astype(
        jnp.bfloat16
    )


def full_transform(half_spec, table_y, width):
    other = jnp.concatenate([half_spec[..., width:], -half_spec[..., :width]], axis=-1)
    stacked = jnp.concatenate([half_spec, other], axis=1)
    return jnp.einsum("uy,iyc->iuc", table_y, stacked, preferred_element_type=jnp.float32).astype(
        jnp.bfloat16
    )


def small_lookup(index_rows, table):
    entries = jnp.arange(table.shape[0], dtype=jnp.int32)
    return jnp.sum(
        jnp.where(index_rows[..., None] == entries, table, jnp.zeros_like(table)), axis=-1
    )


def one_hot(index, count):
    return (index[..., None] == jnp.arange(count, dtype=jnp.int32)).astype(jnp.bfloat16)


def exchange(parts):
    peers = parts[0].shape[0]
    flats = [part.reshape(peers, -1) for part in parts]
    sizes = [flat.shape[1] for flat in flats]
    used = sum(sizes)
    padded = -(-used // 128) * 128
    flats.append(jnp.zeros((peers, padded - used), parts[0].dtype))
    packed = jnp.concatenate(flats, axis=1).reshape(peers, 1, padded)
    moved = lax.all_to_all(packed, "img", split_axis=0, concat_axis=0, tiled=True)
    moved = moved.reshape(peers, padded)
    outs, offset = [], 0
    for part, size in zip(parts, sizes):
        outs.append(moved[:, offset : offset + size].reshape(part.shape))
        offset += size
    return outs


def body(
    images,
    volume,
    row_order,
    tap_owner,
    tap_local,
    interp_index,
    interp_table,
    ctf_index,
    ctf_defocus,
    ctf_phase,
    noise_inv,
):
    f32, bf16, i32 = jnp.float32, jnp.bfloat16, jnp.int32
    image_count, size_k, _ = images.shape
    size_f = size_k // 2
    width = 2 * size_f
    pose_count = row_order.shape[1]
    vol_count = lax.axis_size("vol")
    img_count = lax.axis_size("img")
    quarter = size_k // vol_count
    slab_rows = volume.shape[1]
    slab_index = lax.axis_index("vol")
    row_count = image_count * pose_count * quarter

    table_x, table_y = fourier_tables(size_k, size_f)
    half_spec = half_transform(images, table_x)
    spectrum = full_transform(half_spec, table_y, size_f)
    freq_rows = lax.dynamic_slice_in_dim(row_order, slab_index * quarter, quarter, 2)
    spec_rows = jnp.einsum(
        "ipqu,iuc->ipqc", one_hot(freq_rows, size_k), spectrum, preferred_element_type=f32
    ).astype(bf16).reshape(row_count, width)

    owners = tap_owner[0, ..., 0].reshape(-1)
    local_rows = tap_local[0].reshape(-1)
    request_count = owners.shape[0]
    capacity = request_count * 6 // (5 * img_count) + 2
    slot_count = img_count * capacity
    owner_hot = one_hot(owners, img_count)
    order = jnp.arange(request_count, dtype=i32)
    before = (order[None, :] < order[:, None]).astype(bf16)
    earlier = jnp.dot(before, owner_hot, preferred_element_type=f32)
    rank = jnp.sum(earlier * owner_hot.astype(f32), axis=1).astype(i32)
    slot_of = owners * capacity + rank
    slot_pair = slot_of.reshape(row_count, 2)
    slots = jnp.arange(slot_count, dtype=i32)
    pick_even = (slot_pair[:, 0:1] == slots[None, :]).astype(bf16)
    pick_odd = (slot_pair[:, 1:2] == slots[None, :]).astype(bf16)
    slot_hot_t = (slots[:, None] == slot_of[None, :]).astype(bf16)
    row_of_slot = (
        (slots[:, None] == slot_pair[None, :, 0]) | (slots[:, None] == slot_pair[None, :, 1])
    ).astype(bf16)

    signed_abs = jnp.where(freq_rows < size_f, freq_rows, size_k - freq_rows)
    shape4 = (image_count, pose_count, quarter, 2)
    per_row = lambda a: jnp.broadcast_to(a.reshape(image_count, pose_count, quarter, 1), shape4)
    pose_ids = jnp.broadcast_to(jnp.arange(pose_count, dtype=i32)[None, :, None, None], shape4)
    tap_ids = jnp.broadcast_to(jnp.arange(2, dtype=i32)[None, None, None, :], shape4)
    image_ids = jnp.broadcast_to(jnp.arange(image_count, dtype=i32)[:, None, None, None], shape4)
    ctf_ids = jnp.broadcast_to(ctf_index[:, None, None, None], shape4)
    meta = jnp.stack(
        [
            local_rows.reshape(shape4),
            per_row(signed_abs),
            pose_ids,
            per_row(interp_index[0]),
            tap_ids,
            jnp.ones_like(tap_ids),
            ctf_ids,
            image_ids,
        ],
        axis=-1,
    ).reshape(request_count, -1).astype(bf16)
    meta_count = meta.shape[1]
    send_spec = jnp.dot(row_of_slot, spec_rows, preferred_element_type=f32).astype(bf16)
    send_meta = jnp.dot(slot_hot_t, meta, preferred_element_type=f32).astype(bf16)
    got_spec, got_meta = exchange(
        [send_spec.reshape(img_count, capacity, width), send_meta.reshape(img_count, capacity, meta_count)]
    )
    got_spec = got_spec.reshape(slot_count, width)
    got = got_meta.reshape(slot_count, meta_count).astype(f32).astype(i32)

    got_local, got_abs, got_pose, got_interp = got[:, 0], got[:, 1], got[:, 2], got[:, 3]
    got_tap, got_valid, got_ctf, got_image = got[:, 4], got[:, 5], got[:, 6], got[:, 7]
    row_hot = one_hot(jnp.where(got_valid > 0, got_local, slab_rows), slab_rows)
    found = jnp.dot(row_hot, volume[0], preferred_element_type=f32).astype(bf16)
    (returned,) = exchange([found.reshape(img_count, capacity, width)])
    returned = returned.reshape(slot_count, width)

    defocus = small_lookup(ctf_index, ctf_defocus)[:, None, None, None]
    phase_shift = small_lookup(ctf_index, ctf_phase)[:, None, None, None]
    contrast = contrast_of(signed_abs * signed_abs, defocus, phase_shift, size_f).reshape(
        row_count, size_f
    )
    got_contrast = contrast_of(
        got_abs * got_abs,
        small_lookup(got_ctf, ctf_defocus)[:, None],
        small_lookup(got_ctf, ctf_phase)[:, None],
        size_f,
    )
    returned, contrast, got_contrast = lax.optimization_barrier((returned, contrast, got_contrast))

    tap_even = jnp.dot(pick_even, returned, preferred_element_type=f32).astype(bf16).astype(f32)
    tap_odd = jnp.dot(pick_odd, returned, preferred_element_type=f32).astype(bf16).astype(f32)
    mixing = small_lookup(interp_index[0], interp_table).reshape(row_count, 1)
    sliced = mixing * tap_even + (1.0 - mixing) * tap_odd
    spec_float = spec_rows.astype(f32)
    cross_term = contrast * (
        spec_float[:, :size_f] * sliced[:, :size_f] + spec_float[:, size_f:] * sliced[:, size_f:]
    )
    power_term = contrast * contrast * (sliced[:, :size_f] ** 2 + sliced[:, size_f:] ** 2)
    partial_value = jnp.sum(
        (cross_term - 0.5 * power_term).reshape(image_count, pose_count, quarter * size_f), axis=-1
    )
    score_sum = lax.psum(partial_value, "vol")
    scores = noise_inv[:, None] * score_sum * (1.0 / math.sqrt(size_k * size_f))
    pose_weights = jax.nn.softmax(scores, axis=-1)

    by_peer = lax.all_to_all(
        jnp.broadcast_to(pose_weights.reshape(1, 1, -1), (img_count, 1, image_count * pose_count)),
        "img",
        split_axis=0,
        concat_axis=0,
        tiled=True,
    )
    combo = (got_image * pose_count + got_pose).reshape(img_count, capacity)
    weight_of = jnp.sum(
        jnp.where(
            combo[..., None] == jnp.arange(image_count * pose_count, dtype=i32), by_peer, 0.0
        ),
        axis=-1,
    ).reshape(slot_count)
    mix_of = small_lookup(got_interp, interp_table)
    mix_k = jnp.where(got_tap == 0, mix_of, 1.0 - mix_of)
    coef = mix_k * weight_of
    scaled = coef[:, None] * got_contrast
    got_float = got_spec.astype(f32)
    data_rows = (jnp.concatenate([scaled, scaled], axis=-1) * got_float).astype(bf16)
    weight_rows = (scaled * got_contrast).astype(bf16)
    data_acc = jnp.einsum("sr,sw->rw", row_hot, data_rows, preferred_element_type=f32)
    weight_acc = jnp.einsum("sr,sw->rw", row_hot, weight_rows, preferred_element_type=f32)
    return (data_acc[None], weight_acc[None], pose_weights)


def solution(mesh):
    placed = (
        P("img", None, None),
        P("vol", "img", None),
        P("img", None, None),
        P("vol", "img", None, None, None),
        P("vol", "img", None, None),
        P("vol", "img", None, None),
        P(),
        P("img"),
        P(),
        P(),
        P("img"),
    )
    return jax.shard_map(
        body,
        mesh=mesh,
        in_specs=placed,
        out_specs=(P("vol", "img", None), P("vol", "img", None), P("img", None)),
        check_vma=False,
    )
```

```python
import math

import jax
import jax.numpy as jnp
from jax import lax
from jax.sharding import PartitionSpec as P


def fourier_tables(size_k, size_f):
    positions = jnp.arange(size_k, dtype=jnp.int32)
    columns = jnp.arange(size_f, dtype=jnp.int32)
    scale_factor = 1.0 / math.sqrt(size_k)
    phase_x = (positions[:, None] * columns[None, :] % size_k).astype(jnp.float32) * (
        2.0 * math.pi / size_k
    )
    table_x = jnp.concatenate([jnp.cos(phase_x), -jnp.sin(phase_x)], axis=1) * scale_factor
    phase_y = (positions[:, None] * positions[None, :] % size_k).astype(jnp.float32) * (
        2.0 * math.pi / size_k
    )
    table_y = jnp.concatenate([jnp.cos(phase_y), jnp.sin(phase_y)], axis=1) * scale_factor
    return (table_x.astype(jnp.bfloat16), table_y.astype(jnp.bfloat16))


def contrast_of(radius_sq, defocus, phase_shift, size_f):
    columns = jnp.arange(size_f, dtype=jnp.int32)
    radius = radius_sq[..., None] + columns * columns
    return -jnp.sin(defocus * radius.astype(jnp.float32) + phase_shift)


def half_transform(images, table_x):
    return jnp.einsum("iyx,xc->iyc", images, table_x, preferred_element_type=jnp.float32).astype(
        jnp.bfloat16
    )


def full_transform(half_spec, table_y, width):
    other = jnp.concatenate([half_spec[..., width:], -half_spec[..., :width]], axis=-1)
    stacked = jnp.concatenate([half_spec, other], axis=1)
    return jnp.einsum("uy,iyc->iuc", table_y, stacked, preferred_element_type=jnp.float32).astype(
        jnp.bfloat16
    )


def small_lookup(index_rows, table):
    entries = jnp.arange(table.shape[0], dtype=jnp.int32)
    return jnp.sum(
        jnp.where(index_rows[..., None] == entries, table, jnp.zeros_like(table)), axis=-1
    )


def one_hot(index, count):
    return (index[..., None] == jnp.arange(count, dtype=jnp.int32)).astype(jnp.bfloat16)


def exchange(rows, main_count, over_count):
    peers = rows.shape[0] // (main_count + over_count)
    width = rows.shape[1]
    main = rows[: peers * main_count].reshape(peers, main_count, width)
    spare = -(-width * over_count // main_count)
    over = rows[peers * main_count :].reshape(peers, over_count * width)
    over = jnp.pad(over, ((0, 0), (0, spare * main_count - over_count * width)))
    packed = jnp.concatenate([main, over.reshape(peers, main_count, spare)], axis=2)
    moved = lax.all_to_all(packed, "img", split_axis=0, concat_axis=0, tiled=True)
    got_main = moved[:, :, :width].reshape(peers * main_count, width)
    got_over = moved[:, :, width:].reshape(peers, main_count * spare)[:, : over_count * width]
    return jnp.concatenate([got_main, got_over.reshape(peers * over_count, width)], axis=0)


def body(
    images,
    volume,
    row_order,
    tap_owner,
    tap_local,
    interp_index,
    interp_table,
    ctf_index,
    ctf_defocus,
    ctf_phase,
    noise_inv,
):
    f32, bf16, i32 = jnp.float32, jnp.bfloat16, jnp.int32
    image_count, size_k, _ = images.shape
    size_f = size_k // 2
    width = 2 * size_f
    pose_count = row_order.shape[1]
    vol_count = lax.axis_size("vol")
    img_count = lax.axis_size("img")
    quarter = size_k // vol_count
    slab_rows = volume.shape[1]
    slab_index = lax.axis_index("vol")
    row_count = image_count * pose_count * quarter

    table_x, table_y = fourier_tables(size_k, size_f)
    half_spec = half_transform(images, table_x)
    spectrum = full_transform(half_spec, table_y, size_f)
    freq_rows = lax.dynamic_slice_in_dim(row_order, slab_index * quarter, quarter, 2)
    spec_rows = jnp.einsum(
        "ipqu,iuc->ipqc", one_hot(freq_rows, size_k), spectrum, preferred_element_type=f32
    ).astype(bf16).reshape(row_count, width)

    owners = tap_owner[0, ..., 0].reshape(-1)
    local_rows = tap_local[0].reshape(-1)
    request_count = owners.shape[0]
    capacity = request_count * 6 // (5 * img_count) + 2
    slot_count = img_count * capacity
    owner_hot = one_hot(owners, img_count)
    order = jnp.arange(request_count, dtype=i32)
    before = (order[None, :] < order[:, None]).astype(bf16)
    earlier = jnp.dot(before, owner_hot, preferred_element_type=f32)
    rank = jnp.sum(earlier * owner_hot.astype(f32), axis=1).astype(i32)
    main_count = 16
    over_count = capacity - main_count
    slot_of = jnp.where(
        rank < main_count,
        owners * main_count + rank,
        img_count * main_count + owners * over_count + rank - main_count,
    )
    slot_pair = slot_of.reshape(row_count, 2)
    slots = jnp.arange(slot_count, dtype=i32)
    pick_even = (slot_pair[:, 0:1] == slots[None, :]).astype(bf16)
    pick_odd = (slot_pair[:, 1:2] == slots[None, :]).astype(bf16)
    slot_hot_t = (slots[:, None] == slot_of[None, :]).astype(bf16)
    row_of_slot = (
        (slots[:, None] == slot_pair[None, :, 0]) | (slots[:, None] == slot_pair[None, :, 1])
    ).astype(bf16)

    signed_abs = jnp.where(freq_rows < size_f, freq_rows, size_k - freq_rows)
    shape4 = (image_count, pose_count, quarter, 2)
    per_row = lambda a: jnp.broadcast_to(a.reshape(image_count, pose_count, quarter, 1), shape4)
    pose_ids = jnp.broadcast_to(jnp.arange(pose_count, dtype=i32)[None, :, None, None], shape4)
    tap_ids = jnp.broadcast_to(jnp.arange(2, dtype=i32)[None, None, None, :], shape4)
    image_ids = jnp.broadcast_to(jnp.arange(image_count, dtype=i32)[:, None, None, None], shape4)
    ctf_ids = jnp.broadcast_to(ctf_index[:, None, None, None], shape4)
    meta = jnp.stack(
        [
            local_rows.reshape(shape4),
            per_row(signed_abs),
            pose_ids,
            per_row(interp_index[0]),
            tap_ids,
            jnp.ones_like(tap_ids),
            ctf_ids,
            image_ids,
        ],
        axis=-1,
    ).reshape(request_count, -1).astype(bf16)
    meta_count = meta.shape[1]
    send_spec = jnp.dot(row_of_slot, spec_rows, preferred_element_type=f32).astype(bf16)
    send_meta = jnp.dot(slot_hot_t, meta, preferred_element_type=f32).astype(bf16)
    got_both = exchange(jnp.concatenate([send_spec, send_meta], axis=1), main_count, over_count)
    got_spec = got_both[:, :width]
    got = got_both[:, width:].astype(f32).astype(i32)

    got_local, got_abs, got_pose, got_interp = got[:, 0], got[:, 1], got[:, 2], got[:, 3]
    got_tap, got_valid, got_ctf, got_image = got[:, 4], got[:, 5], got[:, 6], got[:, 7]
    row_hot = one_hot(jnp.where(got_valid > 0, got_local, slab_rows), slab_rows)
    found = jnp.dot(row_hot, volume[0], preferred_element_type=f32).astype(bf16)
    returned = exchange(found, main_count, over_count)

    defocus = small_lookup(ctf_index, ctf_defocus)[:, None, None, None]
    phase_shift = small_lookup(ctf_index, ctf_phase)[:, None, None, None]
    contrast = contrast_of(signed_abs * signed_abs, defocus, phase_shift, size_f).reshape(
        row_count, size_f
    )
    got_contrast = contrast_of(
        got_abs * got_abs,
        small_lookup(got_ctf, ctf_defocus)[:, None],
        small_lookup(got_ctf, ctf_phase)[:, None],
        size_f,
    )
    returned, contrast, got_contrast = lax.optimization_barrier((returned, contrast, got_contrast))

    tap_even = jnp.dot(pick_even, returned, preferred_element_type=f32).astype(bf16).astype(f32)
    tap_odd = jnp.dot(pick_odd, returned, preferred_element_type=f32).astype(bf16).astype(f32)
    mixing = small_lookup(interp_index[0], interp_table).reshape(row_count, 1)
    sliced = mixing * tap_even + (1.0 - mixing) * tap_odd
    spec_float = spec_rows.astype(f32)
    cross_term = contrast * (
        spec_float[:, :size_f] * sliced[:, :size_f] + spec_float[:, size_f:] * sliced[:, size_f:]
    )
    power_term = contrast * contrast * (sliced[:, :size_f] ** 2 + sliced[:, size_f:] ** 2)
    partial_value = jnp.sum(
        (cross_term - 0.5 * power_term).reshape(image_count, pose_count, quarter * size_f), axis=-1
    )
    score_sum = lax.psum(partial_value, "vol")
    scores = noise_inv[:, None] * score_sum * (1.0 / math.sqrt(size_k * size_f))
    pose_weights = jax.nn.softmax(scores, axis=-1)

    by_peer = lax.all_to_all(
        jnp.broadcast_to(pose_weights.reshape(1, 1, -1), (img_count, 1, image_count * pose_count)),
        "img",
        split_axis=0,
        concat_axis=0,
        tiled=True,
    )
    combo = got_image * pose_count + got_pose
    combo_ids = jnp.arange(image_count * pose_count, dtype=i32)
    main_slots = img_count * main_count

    def weight_by_peer(picked, per_peer):
        picked = picked.reshape(img_count, per_peer)
        return jnp.sum(
            jnp.where(picked[..., None] == combo_ids, by_peer, 0.0), axis=-1
        ).reshape(-1)

    weight_of = jnp.concatenate(
        [
            weight_by_peer(combo[:main_slots], main_count),
            weight_by_peer(combo[main_slots:], over_count),
        ]
    )
    mix_of = small_lookup(got_interp, interp_table)
    mix_k = jnp.where(got_tap == 0, mix_of, 1.0 - mix_of)
    coef = mix_k * weight_of
    scaled = coef[:, None] * got_contrast
    got_float = got_spec.astype(f32)
    data_rows = (jnp.concatenate([scaled, scaled], axis=-1) * got_float).astype(bf16)
    weight_rows = (scaled * got_contrast).astype(bf16)
    data_acc = jnp.einsum("sr,sw->rw", row_hot, data_rows, preferred_element_type=f32)
    weight_acc = jnp.einsum("sr,sw->rw", row_hot, weight_rows, preferred_element_type=f32)
    return (data_acc[None], weight_acc[None], pose_weights)


def solution(mesh):
    placed = (
        P("img", None, None),
        P("vol", "img", None),
        P("img", None, None),
        P("vol", "img", None, None, None),
        P("vol", "img", None, None),
        P("vol", "img", None, None),
        P(),
        P("img"),
        P(),
        P(),
        P("img"),
    )
    return jax.shard_map(
        body,
        mesh=mesh,
        in_specs=placed,
        out_specs=(P("vol", "img", None), P("vol", "img", None), P("img", None)),
        check_vma=False,
    )
```

```python
import math

import jax
import jax.numpy as jnp
from jax import lax
from jax.sharding import PartitionSpec as P


def fourier_tables(size_k, size_f):
    positions = jnp.arange(size_k, dtype=jnp.int32)
    columns = jnp.arange(size_f, dtype=jnp.int32)
    scale_factor = 1.0 / math.sqrt(size_k)
    phase_x = (positions[:, None] * columns[None, :] % size_k).astype(jnp.float32) * (
        2.0 * math.pi / size_k
    )
    table_x = jnp.concatenate([jnp.cos(phase_x), -jnp.sin(phase_x)], axis=1) * scale_factor
    phase_y = (positions[:, None] * positions[None, :] % size_k).astype(jnp.float32) * (
        2.0 * math.pi / size_k
    )
    table_y = jnp.concatenate([jnp.cos(phase_y), jnp.sin(phase_y)], axis=1) * scale_factor
    return (table_x.astype(jnp.bfloat16), table_y.astype(jnp.bfloat16))


def contrast_of(radius_sq, defocus, phase_shift, size_f):
    columns = jnp.arange(size_f, dtype=jnp.int32)
    radius = radius_sq[..., None] + columns * columns
    return -jnp.sin(defocus * radius.astype(jnp.float32) + phase_shift)


def half_transform(images, table_x):
    return jnp.einsum("iyx,xc->iyc", images, table_x, preferred_element_type=jnp.float32).astype(
        jnp.bfloat16
    )


def full_transform(half_spec, table_y, width):
    other = jnp.concatenate([half_spec[..., width:], -half_spec[..., :width]], axis=-1)
    stacked = jnp.concatenate([half_spec, other], axis=1)
    return jnp.einsum("uy,iyc->iuc", table_y, stacked, preferred_element_type=jnp.float32).astype(
        jnp.bfloat16
    )


def small_lookup(index_rows, table):
    entries = jnp.arange(table.shape[0], dtype=jnp.int32)
    return jnp.sum(
        jnp.where(index_rows[..., None] == entries, table, jnp.zeros_like(table)), axis=-1
    )


def one_hot(index, count):
    return (index[..., None] == jnp.arange(count, dtype=jnp.int32)).astype(jnp.bfloat16)


def exchange(rows, main_count, over_count):
    peers = rows.shape[0] // (main_count + over_count)
    width = rows.shape[1]
    main = rows[: peers * main_count].reshape(peers, main_count, width)
    spare = -(-width * over_count // main_count)
    over = rows[peers * main_count :].reshape(peers, over_count * width)
    over = jnp.pad(over, ((0, 0), (0, spare * main_count - over_count * width)))
    packed = jnp.concatenate([main, over.reshape(peers, main_count, spare)], axis=2)
    moved = lax.all_to_all(packed, "img", split_axis=0, concat_axis=0, tiled=True)
    got_main = moved[:, :, :width].reshape(peers * main_count, width)
    got_over = moved[:, :, width:].reshape(peers, main_count * spare)[:, : over_count * width]
    return jnp.concatenate([got_main, got_over.reshape(peers * over_count, width)], axis=0)


def body(
    images,
    volume,
    row_order,
    tap_owner,
    tap_local,
    interp_index,
    interp_table,
    ctf_index,
    ctf_defocus,
    ctf_phase,
    noise_inv,
):
    f32, bf16, i32 = jnp.float32, jnp.bfloat16, jnp.int32
    image_count, size_k, _ = images.shape
    size_f = size_k // 2
    width = 2 * size_f
    pose_count = row_order.shape[1]
    vol_count = lax.axis_size("vol")
    img_count = lax.axis_size("img")
    quarter = size_k // vol_count
    slab_rows = volume.shape[1]
    slab_index = lax.axis_index("vol")
    row_count = image_count * pose_count * quarter

    table_x, table_y = fourier_tables(size_k, size_f)
    half_spec = half_transform(images, table_x)
    spectrum = full_transform(half_spec, table_y, size_f)
    freq_rows = lax.dynamic_slice_in_dim(row_order, slab_index * quarter, quarter, 2)
    spec_rows = jnp.einsum(
        "ipqu,iuc->ipqc", one_hot(freq_rows, size_k), spectrum, preferred_element_type=f32
    ).astype(bf16).reshape(row_count, width)

    owners = tap_owner[0, ..., 0].reshape(-1)
    local_rows = tap_local[0].reshape(-1)
    request_count = owners.shape[0]
    capacity = request_count * 6 // (5 * img_count) + 2
    slot_count = img_count * capacity
    owner_hot = one_hot(owners, img_count)
    order = jnp.arange(request_count, dtype=i32)
    before = (order[None, :] < order[:, None]).astype(bf16)
    earlier = jnp.dot(before, owner_hot, preferred_element_type=f32)
    rank = jnp.sum(earlier * owner_hot.astype(f32), axis=1).astype(i32)
    main_count = 16
    over_count = capacity - main_count
    slot_of = jnp.where(
        rank < main_count,
        owners * main_count + rank,
        img_count * main_count + owners * over_count + rank - main_count,
    )
    slot_pair = slot_of.reshape(row_count, 2)
    slots = jnp.arange(slot_count, dtype=i32)
    pick_even = (slot_pair[:, 0:1] == slots[None, :]).astype(bf16)
    pick_odd = (slot_pair[:, 1:2] == slots[None, :]).astype(bf16)
    slot_hot_t = (slots[:, None] == slot_of[None, :]).astype(bf16)
    row_of_slot = (
        (slots[:, None] == slot_pair[None, :, 0]) | (slots[:, None] == slot_pair[None, :, 1])
    ).astype(bf16)

    signed_abs = jnp.where(freq_rows < size_f, freq_rows, size_k - freq_rows)
    shape4 = (image_count, pose_count, quarter, 2)
    per_row = lambda a: jnp.broadcast_to(a.reshape(image_count, pose_count, quarter, 1), shape4)
    pose_ids = jnp.broadcast_to(jnp.arange(pose_count, dtype=i32)[None, :, None, None], shape4)
    tap_ids = jnp.broadcast_to(jnp.arange(2, dtype=i32)[None, None, None, :], shape4)
    image_ids = jnp.broadcast_to(jnp.arange(image_count, dtype=i32)[:, None, None, None], shape4)
    ctf_ids = jnp.broadcast_to(ctf_index[:, None, None, None], shape4)
    meta = jnp.stack(
        [
            local_rows.reshape(shape4),
            per_row(signed_abs),
            pose_ids,
            per_row(interp_index[0]),
            tap_ids,
            jnp.ones_like(tap_ids),
            ctf_ids,
            image_ids,
        ],
        axis=-1,
    ).reshape(request_count, -1).astype(bf16)
    meta_count = meta.shape[1]
    send_spec = jnp.dot(row_of_slot, spec_rows, preferred_element_type=f32).astype(bf16)
    send_meta = jnp.dot(slot_hot_t, meta, preferred_element_type=f32).astype(bf16)
    got_both = exchange(jnp.concatenate([send_spec, send_meta], axis=1), main_count, over_count)
    got_spec = got_both[:, :width]
    got = got_both[:, width:].astype(f32).astype(i32)

    got_local, got_abs, got_pose, got_interp = got[:, 0], got[:, 1], got[:, 2], got[:, 3]
    got_tap, got_valid, got_ctf, got_image = got[:, 4], got[:, 5], got[:, 6], got[:, 7]
    row_hot = one_hot(jnp.where(got_valid > 0, got_local, slab_rows), slab_rows)
    found = jnp.dot(row_hot, volume[0], preferred_element_type=f32).astype(bf16)
    returned = exchange(found, main_count, over_count)

    defocus = small_lookup(ctf_index, ctf_defocus)[:, None, None, None]
    phase_shift = small_lookup(ctf_index, ctf_phase)[:, None, None, None]
    contrast = contrast_of(signed_abs * signed_abs, defocus, phase_shift, size_f).reshape(
        row_count, size_f
    )
    got_contrast = contrast_of(
        got_abs * got_abs,
        small_lookup(got_ctf, ctf_defocus)[:, None],
        small_lookup(got_ctf, ctf_phase)[:, None],
        size_f,
    )
    returned, contrast, got_contrast = lax.optimization_barrier((returned, contrast, got_contrast))

    tap_even = jnp.dot(pick_even, returned, preferred_element_type=f32).astype(bf16).astype(f32)
    tap_odd = jnp.dot(pick_odd, returned, preferred_element_type=f32).astype(bf16).astype(f32)
    mixing = small_lookup(interp_index[0], interp_table).reshape(row_count, 1)
    sliced = mixing * tap_even + (1.0 - mixing) * tap_odd
    spec_float = spec_rows.astype(f32)
    cross_term = contrast * (
        spec_float[:, :size_f] * sliced[:, :size_f] + spec_float[:, size_f:] * sliced[:, size_f:]
    )
    power_term = contrast * contrast * (sliced[:, :size_f] ** 2 + sliced[:, size_f:] ** 2)
    partial_value = jnp.sum(
        (cross_term - 0.5 * power_term).reshape(image_count, pose_count, quarter * size_f), axis=-1
    )
    score_sum = partial_value
    step = 1
    while step < vol_count:
        other = lax.ppermute(score_sum, "vol", [(v, v ^ step) for v in range(vol_count)])
        lower = (slab_index & step) == 0
        score_sum = jnp.where(lower, score_sum, other) + jnp.where(lower, other, score_sum)
        step *= 2
    scores = noise_inv[:, None] * score_sum * (1.0 / math.sqrt(size_k * size_f))
    pose_weights = jax.nn.softmax(scores, axis=-1)

    by_peer = lax.all_to_all(
        jnp.broadcast_to(pose_weights.reshape(1, 1, -1), (img_count, 1, image_count * pose_count)),
        "img",
        split_axis=0,
        concat_axis=0,
        tiled=True,
    )
    combo = got_image * pose_count + got_pose
    combo_ids = jnp.arange(image_count * pose_count, dtype=i32)
    main_slots = img_count * main_count

    def weight_by_peer(picked, per_peer):
        picked = picked.reshape(img_count, per_peer)
        return jnp.sum(
            jnp.where(picked[..., None] == combo_ids, by_peer, 0.0), axis=-1
        ).reshape(-1)

    weight_of = jnp.concatenate(
        [
            weight_by_peer(combo[:main_slots], main_count),
            weight_by_peer(combo[main_slots:], over_count),
        ]
    )
    mix_of = small_lookup(got_interp, interp_table)
    mix_k = jnp.where(got_tap == 0, mix_of, 1.0 - mix_of)
    coef = mix_k * weight_of
    scaled = coef[:, None] * got_contrast
    got_float = got_spec.astype(f32)
    data_rows = (jnp.concatenate([scaled, scaled], axis=-1) * got_float).astype(bf16)
    weight_rows = (scaled * got_contrast).astype(bf16)
    data_acc = jnp.einsum("sr,sw->rw", row_hot, data_rows, preferred_element_type=f32)
    weight_acc = jnp.einsum("sr,sw->rw", row_hot, weight_rows, preferred_element_type=f32)
    return (data_acc[None], weight_acc[None], pose_weights)


def solution(mesh):
    placed = (
        P("img", None, None),
        P("vol", "img", None),
        P("img", None, None),
        P("vol", "img", None, None, None),
        P("vol", "img", None, None),
        P("vol", "img", None, None),
        P(),
        P("img"),
        P(),
        P(),
        P("img"),
    )
    return jax.shard_map(
        body,
        mesh=mesh,
        in_specs=placed,
        out_specs=(P("vol", "img", None), P("vol", "img", None), P("img", None)),
        check_vma=False,
    )
```

```python
import math

import jax
import jax.numpy as jnp
import numpy as np
from jax import lax
from jax.sharding import PartitionSpec as P


def fourier_tables(size_k, size_f):
    positions = np.arange(size_k, dtype=np.int64)
    columns = np.arange(size_f, dtype=np.int64)
    scale_factor = np.float32(1.0 / math.sqrt(size_k))
    step = np.float32(2.0 * math.pi / size_k)
    phase_x = (positions[:, None] * columns[None, :] % size_k).astype(np.float32) * step
    table_x = np.concatenate([np.cos(phase_x), -np.sin(phase_x)], axis=1) * scale_factor
    phase_y = (positions[:, None] * positions[None, :] % size_k).astype(np.float32) * step
    table_y = np.concatenate([np.cos(phase_y), np.sin(phase_y)], axis=1) * scale_factor
    return (
        jnp.asarray(table_x.astype(jnp.bfloat16)),
        jnp.asarray(table_y.astype(jnp.bfloat16)),
    )


def contrast_of(radius_sq, defocus, phase_shift, size_f):
    columns = jnp.arange(size_f, dtype=jnp.int32)
    radius = radius_sq[..., None] + columns * columns
    return -jnp.sin(defocus * radius.astype(jnp.float32) + phase_shift)


def half_transform(images, table_x):
    return jnp.einsum("iyx,xc->iyc", images, table_x, preferred_element_type=jnp.float32).astype(
        jnp.bfloat16
    )


def full_transform(half_spec, table_y, width):
    other = jnp.concatenate([half_spec[..., width:], -half_spec[..., :width]], axis=-1)
    stacked = jnp.concatenate([half_spec, other], axis=1)
    return jnp.einsum("uy,iyc->iuc", table_y, stacked, preferred_element_type=jnp.float32).astype(
        jnp.bfloat16
    )


def small_lookup(index_rows, table):
    entries = jnp.arange(table.shape[0], dtype=jnp.int32)
    return jnp.sum(
        jnp.where(index_rows[..., None] == entries, table, jnp.zeros_like(table)), axis=-1
    )


def one_hot(index, count):
    return (index[..., None] == jnp.arange(count, dtype=jnp.int32)).astype(jnp.bfloat16)


def exchange(rows, main_count, over_count):
    peers = rows.shape[0] // (main_count + over_count)
    width = rows.shape[1]
    main = rows[: peers * main_count].reshape(peers, main_count, width)
    spare = -(-width * over_count // main_count)
    over = rows[peers * main_count :].reshape(peers, over_count * width)
    over = jnp.pad(over, ((0, 0), (0, spare * main_count - over_count * width)))
    packed = jnp.concatenate([main, over.reshape(peers, main_count, spare)], axis=2)
    moved = lax.all_to_all(packed, "img", split_axis=0, concat_axis=0, tiled=True)
    got_main = moved[:, :, :width].reshape(peers * main_count, width)
    got_over = moved[:, :, width:].reshape(peers, main_count * spare)[:, : over_count * width]
    return jnp.concatenate([got_main, got_over.reshape(peers * over_count, width)], axis=0)


def body(
    images,
    volume,
    row_order,
    tap_owner,
    tap_local,
    interp_index,
    interp_table,
    ctf_index,
    ctf_defocus,
    ctf_phase,
    noise_inv,
):
    f32, bf16, i32 = jnp.float32, jnp.bfloat16, jnp.int32
    image_count, size_k, _ = images.shape
    size_f = size_k // 2
    width = 2 * size_f
    pose_count = row_order.shape[1]
    vol_count = lax.axis_size("vol")
    img_count = lax.axis_size("img")
    quarter = size_k // vol_count
    slab_rows = volume.shape[1]
    slab_index = lax.axis_index("vol")
    row_count = image_count * pose_count * quarter

    table_x, table_y = fourier_tables(size_k, size_f)
    half_spec = half_transform(images, table_x)
    spectrum = full_transform(half_spec, table_y, size_f)
    freq_rows = lax.dynamic_slice_in_dim(row_order, slab_index * quarter, quarter, 2)
    spec_rows = jnp.einsum(
        "ipqu,iuc->ipqc", one_hot(freq_rows, size_k), spectrum, preferred_element_type=f32
    ).astype(bf16).reshape(row_count, width)

    owners = tap_owner[0, ..., 0].reshape(-1)
    local_rows = tap_local[0].reshape(-1)
    request_count = owners.shape[0]
    capacity = request_count * 6 // (5 * img_count) + 2
    slot_count = img_count * capacity
    owner_hot = one_hot(owners, img_count)
    order = jnp.arange(request_count, dtype=i32)
    before = (order[None, :] < order[:, None]).astype(bf16)
    earlier = jnp.dot(before, owner_hot, preferred_element_type=f32)
    rank = jnp.sum(earlier * owner_hot.astype(f32), axis=1).astype(i32)
    main_count = 16
    over_count = capacity - main_count
    slot_of = jnp.where(
        rank < main_count,
        owners * main_count + rank,
        img_count * main_count + owners * over_count + rank - main_count,
    )
    slot_pair = slot_of.reshape(row_count, 2)
    slots = jnp.arange(slot_count, dtype=i32)
    pick_even = (slot_pair[:, 0:1] == slots[None, :]).astype(bf16)
    pick_odd = (slot_pair[:, 1:2] == slots[None, :]).astype(bf16)
    slot_hot_t = (slots[:, None] == slot_of[None, :]).astype(bf16)
    row_of_slot = (
        (slots[:, None] == slot_pair[None, :, 0]) | (slots[:, None] == slot_pair[None, :, 1])
    ).astype(bf16)

    signed_abs = jnp.where(freq_rows < size_f, freq_rows, size_k - freq_rows)
    shape4 = (image_count, pose_count, quarter, 2)
    per_row = lambda a: jnp.broadcast_to(a.reshape(image_count, pose_count, quarter, 1), shape4)
    pose_ids = jnp.broadcast_to(jnp.arange(pose_count, dtype=i32)[None, :, None, None], shape4)
    tap_ids = jnp.broadcast_to(jnp.arange(2, dtype=i32)[None, None, None, :], shape4)
    image_ids = jnp.broadcast_to(jnp.arange(image_count, dtype=i32)[:, None, None, None], shape4)
    ctf_ids = jnp.broadcast_to(ctf_index[:, None, None, None], shape4)
    meta = jnp.stack(
        [
            local_rows.reshape(shape4),
            per_row(signed_abs),
            pose_ids,
            per_row(interp_index[0]),
            tap_ids,
            jnp.ones_like(tap_ids),
            ctf_ids,
            image_ids,
        ],
        axis=-1,
    ).reshape(request_count, -1).astype(bf16)
    meta_count = meta.shape[1]
    send_spec = jnp.dot(row_of_slot, spec_rows, preferred_element_type=f32).astype(bf16)
    send_meta = jnp.dot(slot_hot_t, meta, preferred_element_type=f32).astype(bf16)
    got_both = exchange(jnp.concatenate([send_spec, send_meta], axis=1), main_count, over_count)
    got_spec = got_both[:, :width]
    got = got_both[:, width:].astype(f32).astype(i32)

    got_local, got_abs, got_pose, got_interp = got[:, 0], got[:, 1], got[:, 2], got[:, 3]
    got_tap, got_valid, got_ctf, got_image = got[:, 4], got[:, 5], got[:, 6], got[:, 7]
    row_hot = one_hot(jnp.where(got_valid > 0, got_local, slab_rows), slab_rows)
    found = jnp.dot(row_hot, volume[0], preferred_element_type=f32).astype(bf16)
    returned = exchange(found, main_count, over_count)

    defocus = small_lookup(ctf_index, ctf_defocus)[:, None, None, None]
    phase_shift = small_lookup(ctf_index, ctf_phase)[:, None, None, None]
    contrast = contrast_of(signed_abs * signed_abs, defocus, phase_shift, size_f).reshape(
        row_count, size_f
    )
    got_contrast = contrast_of(
        got_abs * got_abs,
        small_lookup(got_ctf, ctf_defocus)[:, None],
        small_lookup(got_ctf, ctf_phase)[:, None],
        size_f,
    )
    returned, contrast, got_contrast = lax.optimization_barrier((returned, contrast, got_contrast))

    tap_even = jnp.dot(pick_even, returned, preferred_element_type=f32).astype(bf16).astype(f32)
    tap_odd = jnp.dot(pick_odd, returned, preferred_element_type=f32).astype(bf16).astype(f32)
    mixing = small_lookup(interp_index[0], interp_table).reshape(row_count, 1)
    sliced = mixing * tap_even + (1.0 - mixing) * tap_odd
    spec_float = spec_rows.astype(f32)
    cross_term = contrast * (
        spec_float[:, :size_f] * sliced[:, :size_f] + spec_float[:, size_f:] * sliced[:, size_f:]
    )
    power_term = contrast * contrast * (sliced[:, :size_f] ** 2 + sliced[:, size_f:] ** 2)
    partial_value = jnp.sum(
        (cross_term - 0.5 * power_term).reshape(image_count, pose_count, quarter * size_f), axis=-1
    )
    score_sum = partial_value
    step = 1
    while step < vol_count:
        other = lax.ppermute(score_sum, "vol", [(v, v ^ step) for v in range(vol_count)])
        lower = (slab_index & step) == 0
        score_sum = jnp.where(lower, score_sum, other) + jnp.where(lower, other, score_sum)
        step *= 2
    scores = noise_inv[:, None] * score_sum * (1.0 / math.sqrt(size_k * size_f))
    pose_weights = jax.nn.softmax(scores, axis=-1)

    by_peer = lax.all_to_all(
        jnp.broadcast_to(pose_weights.reshape(1, 1, -1), (img_count, 1, image_count * pose_count)),
        "img",
        split_axis=0,
        concat_axis=0,
        tiled=True,
    )
    combo = got_image * pose_count + got_pose
    combo_ids = jnp.arange(image_count * pose_count, dtype=i32)
    main_slots = img_count * main_count

    def weight_by_peer(picked, per_peer):
        picked = picked.reshape(img_count, per_peer)
        return jnp.sum(
            jnp.where(picked[..., None] == combo_ids, by_peer, 0.0), axis=-1
        ).reshape(-1)

    weight_of = jnp.concatenate(
        [
            weight_by_peer(combo[:main_slots], main_count),
            weight_by_peer(combo[main_slots:], over_count),
        ]
    )
    mix_of = small_lookup(got_interp, interp_table)
    mix_k = jnp.where(got_tap == 0, mix_of, 1.0 - mix_of)
    coef = mix_k * weight_of
    scaled = coef[:, None] * got_contrast
    got_float = got_spec.astype(f32)
    data_rows = (jnp.concatenate([scaled, scaled], axis=-1) * got_float).astype(bf16)
    weight_rows = (scaled * got_contrast).astype(bf16)
    data_acc = jnp.einsum("sr,sw->rw", row_hot, data_rows, preferred_element_type=f32)
    weight_acc = jnp.einsum("sr,sw->rw", row_hot, weight_rows, preferred_element_type=f32)
    return (data_acc[None], weight_acc[None], pose_weights)


def solution(mesh):
    placed = (
        P("img", None, None),
        P("vol", "img", None),
        P("img", None, None),
        P("vol", "img", None, None, None),
        P("vol", "img", None, None),
        P("vol", "img", None, None),
        P(),
        P("img"),
        P(),
        P(),
        P("img"),
    )
    return jax.shard_map(
        body,
        mesh=mesh,
        in_specs=placed,
        out_specs=(P("vol", "img", None), P("vol", "img", None), P("img", None)),
        check_vma=False,
    )
```

```python
import math

import jax
import jax.numpy as jnp
import numpy as np
from jax import lax
from jax.sharding import PartitionSpec as P


def fourier_tables(size_k, size_f):
    positions = np.arange(size_k, dtype=np.int64)
    columns = np.arange(size_f, dtype=np.int64)
    scale_factor = np.float32(1.0 / math.sqrt(size_k))
    step = np.float32(2.0 * math.pi / size_k)
    phase_x = (positions[:, None] * columns[None, :] % size_k).astype(np.float32) * step
    table_x = np.concatenate([np.cos(phase_x), -np.sin(phase_x)], axis=1) * scale_factor
    phase_y = (positions[:, None] * positions[None, :] % size_k).astype(np.float32) * step
    table_y = np.concatenate([np.cos(phase_y), np.sin(phase_y)], axis=1) * scale_factor
    return (
        jnp.asarray(table_x.astype(jnp.bfloat16)),
        jnp.asarray(table_y.astype(jnp.bfloat16)),
    )


def contrast_of(radius_sq, defocus, phase_shift, size_f):
    columns = jnp.arange(size_f, dtype=jnp.int32)
    radius = radius_sq[..., None] + columns * columns
    return -jnp.sin(defocus * radius.astype(jnp.float32) + phase_shift)


def half_transform(images, table_x):
    return jnp.einsum("iyx,xc->iyc", images, table_x, preferred_element_type=jnp.float32).astype(
        jnp.bfloat16
    )


def full_transform(half_spec, table_y, width):
    other = jnp.concatenate([half_spec[..., width:], -half_spec[..., :width]], axis=-1)
    stacked = jnp.concatenate([half_spec, other], axis=1)
    return jnp.einsum("uy,iyc->iuc", table_y, stacked, preferred_element_type=jnp.float32).astype(
        jnp.bfloat16
    )


def small_lookup(index_rows, table):
    entries = jnp.arange(table.shape[0], dtype=jnp.int32)
    return jnp.sum(
        jnp.where(index_rows[..., None] == entries, table, jnp.zeros_like(table)), axis=-1
    )


def one_hot(index, count):
    return (index[..., None] == jnp.arange(count, dtype=jnp.int32)).astype(jnp.bfloat16)


def exchange(rows, main_count, over_count, split=False):
    peers = rows.shape[0] // (main_count + over_count)
    width = rows.shape[1]
    main = rows[: peers * main_count].reshape(peers, main_count, width)
    spare = -(-width * over_count // main_count)
    over = rows[peers * main_count :].reshape(peers, over_count * width)
    over = jnp.pad(over, ((0, 0), (0, spare * main_count - over_count * width)))
    packed = jnp.concatenate([main, over.reshape(peers, main_count, spare)], axis=2)
    moved = lax.all_to_all(packed, "img", split_axis=0, concat_axis=0, tiled=True)
    got_main = moved[:, :, :width].reshape(peers * main_count, width)
    got_over = moved[:, :, width:].reshape(peers, main_count * spare)[:, : over_count * width]
    if split:
        return got_main, got_over.reshape(peers * over_count, width)
    return jnp.concatenate([got_main, got_over.reshape(peers * over_count, width)], axis=0)


def body(
    images,
    volume,
    row_order,
    tap_owner,
    tap_local,
    interp_index,
    interp_table,
    ctf_index,
    ctf_defocus,
    ctf_phase,
    noise_inv,
):
    f32, bf16, i32 = jnp.float32, jnp.bfloat16, jnp.int32
    image_count, size_k, _ = images.shape
    size_f = size_k // 2
    width = 2 * size_f
    pose_count = row_order.shape[1]
    vol_count = lax.axis_size("vol")
    img_count = lax.axis_size("img")
    quarter = size_k // vol_count
    slab_rows = volume.shape[1]
    slab_index = lax.axis_index("vol")
    row_count = image_count * pose_count * quarter

    table_x, table_y = fourier_tables(size_k, size_f)
    half_spec = half_transform(images, table_x)
    spectrum = full_transform(half_spec, table_y, size_f)
    freq_rows = lax.dynamic_slice_in_dim(row_order, slab_index * quarter, quarter, 2)
    spec_rows = jnp.einsum(
        "ipqu,iuc->ipqc", one_hot(freq_rows, size_k), spectrum, preferred_element_type=f32
    ).astype(bf16).reshape(row_count, width)

    owners = tap_owner[0, ..., 0].reshape(-1)
    local_rows = tap_local[0].reshape(-1)
    request_count = owners.shape[0]
    capacity = request_count * 6 // (5 * img_count) + 2
    slot_count = img_count * capacity
    owner_hot = one_hot(owners, img_count)
    order = jnp.arange(request_count, dtype=i32)
    before = (order[None, :] < order[:, None]).astype(bf16)
    earlier = jnp.dot(before, owner_hot, preferred_element_type=f32)
    rank = jnp.sum(earlier * owner_hot.astype(f32), axis=1).astype(i32)
    main_count = 16
    over_count = capacity - main_count
    slot_of = jnp.where(
        rank < main_count,
        owners * main_count + rank,
        img_count * main_count + owners * over_count + rank - main_count,
    )
    slot_pair = slot_of.reshape(row_count, 2)
    slots = jnp.arange(slot_count, dtype=i32)
    pick_even = (slot_pair[:, 0:1] == slots[None, :]).astype(bf16)
    pick_odd = (slot_pair[:, 1:2] == slots[None, :]).astype(bf16)
    slot_hot_t = (slots[:, None] == slot_of[None, :]).astype(bf16)
    row_of_slot = (
        (slots[:, None] == slot_pair[None, :, 0]) | (slots[:, None] == slot_pair[None, :, 1])
    ).astype(bf16)

    signed_abs = jnp.where(freq_rows < size_f, freq_rows, size_k - freq_rows)
    shape4 = (image_count, pose_count, quarter, 2)
    per_row = lambda a: jnp.broadcast_to(a.reshape(image_count, pose_count, quarter, 1), shape4)
    pose_ids = jnp.broadcast_to(jnp.arange(pose_count, dtype=i32)[None, :, None, None], shape4)
    tap_ids = jnp.broadcast_to(jnp.arange(2, dtype=i32)[None, None, None, :], shape4)
    image_ids = jnp.broadcast_to(jnp.arange(image_count, dtype=i32)[:, None, None, None], shape4)
    ctf_ids = jnp.broadcast_to(ctf_index[:, None, None, None], shape4)
    meta = jnp.stack(
        [
            local_rows.reshape(shape4),
            per_row(signed_abs),
            pose_ids,
            per_row(interp_index[0]),
            tap_ids,
            jnp.ones_like(tap_ids),
            ctf_ids,
            image_ids,
        ],
        axis=-1,
    ).reshape(request_count, -1).astype(bf16)
    meta_count = meta.shape[1]
    send_spec = jnp.dot(row_of_slot, spec_rows, preferred_element_type=f32).astype(bf16)
    send_meta = jnp.dot(slot_hot_t, meta, preferred_element_type=f32).astype(bf16)
    got_both = exchange(jnp.concatenate([send_spec, send_meta], axis=1), main_count, over_count)
    got_spec = got_both[:, :width]
    got = got_both[:, width:].astype(f32).astype(i32)

    got_local, got_abs, got_pose, got_interp = got[:, 0], got[:, 1], got[:, 2], got[:, 3]
    got_tap, got_valid, got_ctf, got_image = got[:, 4], got[:, 5], got[:, 6], got[:, 7]
    row_hot = one_hot(jnp.where(got_valid > 0, got_local, slab_rows), slab_rows)
    found = jnp.dot(row_hot, volume[0], preferred_element_type=f32).astype(bf16)
    returned_main, returned_over = exchange(found, main_count, over_count, split=True)

    defocus = small_lookup(ctf_index, ctf_defocus)[:, None, None, None]
    phase_shift = small_lookup(ctf_index, ctf_phase)[:, None, None, None]
    contrast = contrast_of(signed_abs * signed_abs, defocus, phase_shift, size_f).reshape(
        row_count, size_f
    )
    got_contrast = contrast_of(
        got_abs * got_abs,
        small_lookup(got_ctf, ctf_defocus)[:, None],
        small_lookup(got_ctf, ctf_phase)[:, None],
        size_f,
    )
    returned_main, returned_over, contrast, got_contrast = lax.optimization_barrier(
        (returned_main, returned_over, contrast, got_contrast)
    )

    split_at = img_count * main_count

    def gather_taps(pick):
        return (
            jnp.dot(pick[:, :split_at], returned_main, preferred_element_type=f32)
            + jnp.dot(pick[:, split_at:], returned_over, preferred_element_type=f32)
        ).astype(bf16).astype(f32)

    tap_even = gather_taps(pick_even)
    tap_odd = gather_taps(pick_odd)
    mixing = small_lookup(interp_index[0], interp_table).reshape(row_count, 1)
    sliced = mixing * tap_even + (1.0 - mixing) * tap_odd
    spec_float = spec_rows.astype(f32)
    cross_term = contrast * (
        spec_float[:, :size_f] * sliced[:, :size_f] + spec_float[:, size_f:] * sliced[:, size_f:]
    )
    power_term = contrast * contrast * (sliced[:, :size_f] ** 2 + sliced[:, size_f:] ** 2)
    partial_value = jnp.sum(
        (cross_term - 0.5 * power_term).reshape(image_count, pose_count, quarter * size_f), axis=-1
    )
    score_sum = partial_value
    step = 1
    while step < vol_count:
        other = lax.ppermute(score_sum, "vol", [(v, v ^ step) for v in range(vol_count)])
        lower = (slab_index & step) == 0
        score_sum = jnp.where(lower, score_sum, other) + jnp.where(lower, other, score_sum)
        step *= 2
    scores = noise_inv[:, None] * score_sum * (1.0 / math.sqrt(size_k * size_f))
    pose_weights = jax.nn.softmax(scores, axis=-1)

    by_peer = lax.all_to_all(
        jnp.broadcast_to(pose_weights.reshape(1, 1, -1), (img_count, 1, image_count * pose_count)),
        "img",
        split_axis=0,
        concat_axis=0,
        tiled=True,
    )
    combo = got_image * pose_count + got_pose
    combo_ids = jnp.arange(image_count * pose_count, dtype=i32)
    main_slots = img_count * main_count

    def weight_by_peer(picked, per_peer):
        picked = picked.reshape(img_count, per_peer)
        return jnp.sum(
            jnp.where(picked[..., None] == combo_ids, by_peer, 0.0), axis=-1
        ).reshape(-1)

    weight_of = jnp.concatenate(
        [
            weight_by_peer(combo[:main_slots], main_count),
            weight_by_peer(combo[main_slots:], over_count),
        ]
    )
    mix_of = small_lookup(got_interp, interp_table)
    mix_k = jnp.where(got_tap == 0, mix_of, 1.0 - mix_of)
    coef = mix_k * weight_of
    scaled = coef[:, None] * got_contrast
    got_float = got_spec.astype(f32)
    data_rows = (jnp.concatenate([scaled, scaled], axis=-1) * got_float).astype(bf16)
    weight_rows = (scaled * got_contrast).astype(bf16)
    data_acc = jnp.einsum("sr,sw->rw", row_hot, data_rows, preferred_element_type=f32)
    weight_acc = jnp.einsum("sr,sw->rw", row_hot, weight_rows, preferred_element_type=f32)
    return (data_acc[None], weight_acc[None], pose_weights)


def solution(mesh):
    placed = (
        P("img", None, None),
        P("vol", "img", None),
        P("img", None, None),
        P("vol", "img", None, None, None),
        P("vol", "img", None, None),
        P("vol", "img", None, None),
        P(),
        P("img"),
        P(),
        P(),
        P("img"),
    )
    return jax.shard_map(
        body,
        mesh=mesh,
        in_specs=placed,
        out_specs=(P("vol", "img", None), P("vol", "img", None), P("img", None)),
        check_vma=False,
    )
```
